256 devices in a mesh: seq: 128 (over z, y, x_lo, core), dp: 2 (over x_hi).
Axes of the slice: x: 4 (x_hi: 2, x_lo: 2; x = x_hi * 2 + x_lo), y: 4, z: 8, core: 2. Of those that a mesh axis runs over, the one named last changes fastest.
Arguments:
- frames: bfloat16 [2, 16384, 1024], P('dp', 'seq'), may hold values from -36 to 36
- kernel: bfloat16 [31, 1024], replicated, may hold values from -1 to 1
- norm_gain: float32 [1024], replicated, may hold values from 0.5 to 1.5
- router: bfloat16 [1024, 32], replicated, may hold values from -0.1875 to 0.1875
- experts: int32 [2, 16384, 2], P('dp', 'seq'), may hold values from 0 to 31, all different within a row; in each aligned block of 128 rows (0 to 127, 128 to 255, ..., all dimensions but the last counted through in order) at most 16 rows name the same one
- w_in: bfloat16 [128, 1024, 512], P('seq'), may hold values from -0.1875 to 0.1875
- w_out: bfloat16 [128, 512, 1024], P('seq'), may hold values from -0.125 to 0.125
- cotangent: bfloat16 [2, 16384, 1024], P('dp', 'seq'), may hold values from -8 to 8
Outputs:
- mixed: bfloat16 [2, 16384, 1024], P('dp', 'seq')
- grad_frames: bfloat16 [2, 16384, 1024], P('dp', 'seq')
- grad_kernel: float32 [31, 1024], replicated
- grad_gain: float32 [1024], replicated
- grad_router: float32 [1024, 32], replicated
- grad_w_in: float32 [128, 1024, 512], P('seq')
- grad_w_out: float32 [128, 512, 1024], P('seq')
The draws below stay inside these ranges and needn't reach their ends.
Inputs may be any that keep to these rules, and one draw needn't show every extreme that they name: Each frame names 2 different experts; in each aligned block of 128 frames no expert is named more than 16 times, a bound that some block reaches.
All inputs are finite; a program needn't handle non-finite values.
Results may differ from the reference program's by a relative error of at most 0.0075.
Values may be sent and summed in bfloat16 or wider, within the bound.
No kernel may reach another device: no remote copies, remote signals or barrier semaphores. Data moves between devices by JAX's collectives and lax.ppermute only.
A program may use at most 128 MiB of HBM per device.

```python
import math
import jax
import jax.numpy as jnp
import numpy as np
from jax import lax

D = 1024
FF = 2048
KW = 31
TOP = 2
GROUP = 4
TOK_DEV = 128
EXPERTS = 32
HID_DEV = 512
CAP = 16
FRAMES = 16384
RECS = 2
N_SEQ = 128


def draw_frames(key, part):
    first_key, row_key, col_key = jax.random.split(key, 3)
    values = jnp.clip(jax.random.normal(first_key, (RECS, FRAMES, D), jnp.float32), -4.0, 4.0)
    row_scale = jnp.exp(jax.random.uniform(row_key, (RECS, FRAMES, 1), jnp.float32, math.log(0.3), math.log(3.0)))
    col_scale = jnp.exp(jax.random.uniform(col_key, (1, 1, D), jnp.float32, math.log(0.3), math.log(3.0)))
    return (values * row_scale * col_scale).astype(jnp.bfloat16)


def draw_cotangent(key, part):
    first_key = jax.random.fold_in(key, 0)
    values = jnp.clip(jax.random.normal(first_key, (RECS, FRAMES, D), jnp.float32), -4.0, 4.0)
    ramp = 0.5 + 1.5 * jnp.arange(FRAMES, dtype=jnp.float32) / FRAMES
    return (values * ramp[None, :, None]).astype(jnp.bfloat16)


def shard_levels(rng, extent, pieces, least, largest):
    def one(axis_at, parts):
        draws = jax.random.uniform(jax.random.fold_in(jax.random.fold_in(rng, 6), axis_at), (parts,), jnp.float32, least / len(pieces), largest / len(pieces))
        return jnp.repeat(jnp.exp(draws), extent[axis_at] // parts).reshape((-1,) + (1,) * (len(extent) - axis_at - 1))

    loudness = one(*pieces[0])
    for cut in pieces[1:]:
        loudness = loudness * one(*cut)
    return loudness


def routed_block(key, own, number, rows, amount, top, most, lean):
    order = jax.random.permutation(key, amount)
    heavy_load, ordinary = load_shares(amount, rows * top, most, lean, True), load_shares(amount, rows * top, most, lean, False)
    places = jnp.arange(amount)

    def named(sizes, turn):
        used = int((sizes > 0).sum())
        fixed = max(1, used // 4)
        passed = fixed + (places - fixed + turn * (used - fixed)) % max(1, amount - fixed)
        return jnp.zeros((amount,), jnp.int32).at[order[jnp.where(places < fixed, places, passed)]].set(jnp.asarray(sizes, jnp.int32))

    sizes = jnp.where(number % 4 == 0, named(heavy_load, number // 4), named(ordinary, number - number // 4 - 1))
    mixed = jax.random.permutation(jax.random.fold_in(own, 3), amount)
    donor, sink = mixed[0:amount // 2 * 2:2], mixed[1:amount // 2 * 2:2]
    slack = jnp.minimum(sizes[donor] - 1, most - sizes[sink]) // 2
    slack = jnp.where((donor == order[0]) | (sink == order[0]) | (sizes[sink] == 0), 0, jnp.maximum(slack, 0))
    passed = jax.random.randint(jax.random.fold_in(own, 4), (amount // 2,), 0, 1 << 20) % (slack + 1)
    sizes = sizes.at[donor].add(-passed).at[sink].add(passed)
    members = jnp.searchsorted(jnp.cumsum(sizes), jnp.arange(rows * top), side="right").astype(jnp.int32)
    grid = members.reshape(top, rows).T
    grid = grid[jax.random.permutation(jax.random.fold_in(own, 1), rows)]
    turn = jax.random.randint(jax.random.fold_in(own, 2), (rows, 1), 0, top)
    return jnp.take_along_axis(grid, (jnp.arange(top)[None, :] + turn) % top, axis=1)


def load_shares(amount, total, limit, skew, full):
    portions = [(1 << 20) // math.isqrt(grade ** skew) + 1 for grade in range(1, amount + 1)]
    largest = limit if full else min(limit, max(-(-total // amount), total * portions[0] // sum(portions)))
    least = 1 if total - largest >= amount - 1 else 0
    counts, spare = [largest] + [least] * (amount - 1), total - largest - least * (amount - 1)
    while spare > 0:
        free = [i for i in range(1, amount) if counts[i] < largest] or [i for i in range(1, amount) if counts[i] < limit]
        pool, left = sum([portions[i] for i in free]), spare
        for i in free:
            extra = min(limit - counts[i], max(1, left * portions[i] // pool), spare)
            counts[i] = counts[i] + extra
            spare = spare - extra
    return np.array(counts)


def gaussian(own_key, shape, spread, most, cuts=(), kind=jnp.bfloat16):
    drawn = spread * jax.random.normal(own_key, shape, jnp.float32)
    if cuts:
        drawn = drawn * shard_levels(own_key, shape, cuts, -0.22, 0.18)
    return jnp.clip(drawn, -most, most).astype(kind)


def setup_inputs(seed: int = 0) -> dict:
    streams_of = jax.random.split(jax.random.key(seed), 9)
    frames = draw_frames(jax.random.fold_in(streams_of[8], 71), 0)
    kernel = gaussian(streams_of[1], (KW, D), KW ** -0.5, 1.0)
    norm_gain = jnp.clip(1.0 + 0.1 * jax.random.normal(streams_of[2], (D,), jnp.float32), 0.5, 1.5)
    router = gaussian(streams_of[3], (D, EXPERTS), D ** -0.5, 0.1875)
    experts_keys = jax.random.split(jax.random.fold_in(streams_of[4], 1), RECS * FRAMES // TOK_DEV)
    experts_turns = jax.random.permutation(jax.random.fold_in(streams_of[4], 3), RECS * FRAMES // TOK_DEV)
    experts = jax.vmap(lambda own, number: routed_block(jax.random.fold_in(streams_of[4], 2), own, number, TOK_DEV, EXPERTS, TOP, CAP, 2))(experts_keys, experts_turns).reshape((RECS, FRAMES, TOP))
    w_in = gaussian(streams_of[5], (N_SEQ, D, HID_DEV), D ** -0.5, 0.1875, ((0, 128),))
    w_out = gaussian(streams_of[6], (N_SEQ, HID_DEV, D), FF ** -0.5, 0.125, ((0, 128),))
    cotangent = draw_cotangent(jax.random.fold_in(streams_of[8], 71), 0)
    return dict(frames=frames, kernel=kernel, norm_gain=norm_gain, router=router, experts=experts, w_in=w_in, w_out=w_out, cotangent=cotangent)


eps = 1e-06

def conv_forward(padded, kernel, row_count):
    summed = jnp.zeros((row_count, padded.shape[1]), jnp.float32)
    for offset in range(kernel.shape[0]):
        summed = summed + kernel[offset].astype(jnp.float32) * padded[offset:offset + row_count].astype(jnp.float32)
    return summed

def conv_transpose(padded, kernel, row_count):
    length = kernel.shape[0]
    summed = jnp.zeros((row_count, padded.shape[1]), jnp.float32)
    for offset in range(length):
        start = length - 1 - offset
        summed = summed + kernel[offset].astype(jnp.float32) * padded[start:start + row_count]
    return summed

def kernel_terms(padded, upstream, length, row_count):
    return jnp.stack([lax.optimization_barrier(jnp.sum(padded[offset:offset + row_count].astype(jnp.float32) * upstream, axis=0)) for offset in range(length)])

def normalize(summed, norm_gain):
    square = lax.optimization_barrier(jnp.mean(summed * summed, axis=-1, keepdims=True))
    return summed * lax.rsqrt(square + eps) * norm_gain

def slot_numbers(expert_ids, expert_count):
    onehot = (expert_ids[:, None] == jnp.arange(expert_count, dtype=jnp.int32)[None, :]).astype(jnp.int32)
    ranks = jnp.cumsum(onehot, axis=0) - onehot
    return lax.optimization_barrier(jnp.sum(ranks * onehot, axis=1)).astype(jnp.int32)

def gate_values(normed_b, router, first_ids, second_ids):
    logits = jnp.dot(normed_b, router, preferred_element_type=jnp.float32)
    columns = jnp.arange(router.shape[1], dtype=jnp.int32)[None, :]
    pick_diff = (first_ids[:, None] == columns).astype(jnp.float32) - (second_ids[:, None] == columns).astype(jnp.float32)
    gate_one = jax.nn.sigmoid(lax.optimization_barrier(jnp.sum(logits * pick_diff, axis=1)))
    return (gate_one, 1.0 - gate_one, pick_diff)

def swish_parts(pre_act):
    squash = jax.nn.sigmoid(pre_act)
    return (pre_act * squash, squash * (1.0 + pre_act * (1.0 - squash)))

def gate_backward(upstream, out_one, out_two, gate_one, gate_two, pick_diff, normed_b, router):
    grad_gap = (lax.optimization_barrier(jnp.sum(upstream * out_one, axis=1)) - lax.optimization_barrier(jnp.sum(upstream * out_two, axis=1))) * gate_one * gate_two
    grad_logits = (grad_gap[:, None] * pick_diff).astype(jnp.bfloat16)
    router_term = jnp.dot(normed_b.T, grad_logits, preferred_element_type=jnp.float32)
    normed_term = jnp.dot(grad_logits, router.T, preferred_element_type=jnp.float32)
    return (router_term, normed_term)

def reference(frames, kernel, norm_gain, router, experts, w_in, w_out, cotangent):
    half_width = KW // 2
    group_rows = N_SEQ * CAP
    assign_count = FRAMES * TOP
    outputs = []
    frame_grads = []
    grad_kernel = jnp.zeros((KW, D), jnp.float32)
    grad_gain = jnp.zeros((D,), jnp.float32)
    grad_router = jnp.zeros((D, EXPERTS), jnp.float32)
    grad_in = jnp.zeros((N_SEQ, D, HID_DEV), jnp.float32)
    grad_out = jnp.zeros((N_SEQ, HID_DEV, D), jnp.float32)
    for recording in range(RECS):
        inputs_rec = frames[recording]
        padded = jnp.pad(inputs_rec, ((half_width, half_width), (0, 0)))
        summed = inputs_rec.astype(jnp.float32) + conv_forward(padded, kernel, FRAMES)
        normed_b = normalize(summed, norm_gain).astype(jnp.bfloat16)
        choice_ids = experts[recording]
        gate_one, gate_two, pick_diff = gate_values(normed_b, router, choice_ids[:, 0], choice_ids[:, 1])
        block_ids = choice_ids.reshape(N_SEQ, TOK_DEV * TOP)
        block_slots = jax.vmap(lambda values: slot_numbers(values, EXPERTS))(block_ids)
        sources = jnp.arange(N_SEQ, dtype=jnp.int32)[:, None]
        position = (sources * CAP + block_slots).reshape(-1).astype(jnp.int32)
        flat_ids = block_ids.reshape(-1)
        lookup = jnp.full((EXPERTS, group_rows), assign_count, jnp.int32)
        lookup = lookup.at[flat_ids, position].set(jnp.arange(assign_count, dtype=jnp.int32))
        gather_index = (flat_ids * group_rows + position).astype(jnp.int32)
        spread_rows = jnp.concatenate([jnp.repeat(normed_b, TOP, axis=0), jnp.zeros((1, D), jnp.bfloat16)], axis=0)

        def expert_forward(expert):
            arrived = jnp.take(spread_rows, lookup[expert], axis=0)
            in_block = lax.dynamic_slice_in_dim(w_in, (expert * GROUP).astype(jnp.int32), GROUP, 0)
            out_block = lax.dynamic_slice_in_dim(w_out, (expert * GROUP).astype(jnp.int32), GROUP, 0)
            combined = jnp.zeros((group_rows, D), jnp.float32)
            for member in range(GROUP):
                pre_act = jnp.dot(arrived, in_block[member], preferred_element_type=jnp.float32)
                hidden = swish_parts(pre_act)[0].astype(jnp.bfloat16)
                partial_out = jnp.dot(hidden, out_block[member], preferred_element_type=jnp.float32)
                combined = combined + lax.optimization_barrier(partial_out.astype(jnp.bfloat16)).astype(jnp.float32)
            return combined
        expert_out = lax.map(expert_forward, jnp.arange(EXPERTS, dtype=jnp.int32)).reshape(EXPERTS * group_rows, D)
        assigned = jnp.take(expert_out, gather_index, axis=0).reshape(FRAMES, TOP, D)
        out_one = assigned[:, 0]
        out_two = assigned[:, 1]
        outputs.append((summed + gate_one[:, None] * out_one + gate_two[:, None] * out_two).astype(jnp.bfloat16))
        upstream = cotangent[recording].astype(jnp.float32)
        grad_assigned = jnp.stack([gate_one[:, None] * upstream, gate_two[:, None] * upstream], axis=1)
        grad_assigned = grad_assigned.reshape(assign_count, D).astype(jnp.bfloat16)
        spread_grads = jnp.concatenate([grad_assigned, jnp.zeros((1, D), jnp.bfloat16)], axis=0)

        def expert_backward(expert):
            arrived = jnp.take(spread_rows, lookup[expert], axis=0)
            incoming = jnp.take(spread_grads, lookup[expert], axis=0)
            in_block = lax.dynamic_slice_in_dim(w_in, (expert * GROUP).astype(jnp.int32), GROUP, 0)
            out_block = lax.dynamic_slice_in_dim(w_out, (expert * GROUP).astype(jnp.int32), GROUP, 0)
            grad_rows = jnp.zeros((group_rows, D), jnp.float32)
            in_terms = []
            out_terms = []
            for member in range(GROUP):
                pre_act = jnp.dot(arrived, in_block[member], preferred_element_type=jnp.float32)
                hidden_f, slope = swish_parts(pre_act)
                hidden = hidden_f.astype(jnp.bfloat16)
                grad_hidden = jnp.dot(incoming, out_block[member].T, preferred_element_type=jnp.float32)
                grad_pre = (grad_hidden * slope).astype(jnp.bfloat16)
                out_terms.append(jnp.dot(hidden.T, incoming, preferred_element_type=jnp.float32))
                in_terms.append(jnp.dot(arrived.T, grad_pre, preferred_element_type=jnp.float32))
                grad_part = jnp.dot(grad_pre, in_block[member].T, preferred_element_type=jnp.float32)
                grad_rows = grad_rows + lax.optimization_barrier(grad_part.astype(jnp.bfloat16)).astype(jnp.float32)
            return (grad_rows, jnp.stack(in_terms), jnp.stack(out_terms))
        grad_rows, in_terms, out_terms = lax.map(expert_backward, jnp.arange(EXPERTS, dtype=jnp.int32))
        grad_in = grad_in + in_terms.reshape(N_SEQ, D, HID_DEV)
        grad_out = grad_out + out_terms.reshape(N_SEQ, HID_DEV, D)
        normed_grads = jnp.take(grad_rows.reshape(EXPERTS * group_rows, D), gather_index, axis=0)
        normed_grads = lax.optimization_barrier(jnp.sum(normed_grads.reshape(FRAMES, TOP, D), axis=1))
        router_term, normed_term = gate_backward(upstream, out_one, out_two, gate_one, gate_two, pick_diff, normed_b, router)
        pullback = jax.vjp(normalize, summed, norm_gain)[1]
        summed_grad, gain_term = pullback(normed_grads + normed_term)
        upstream_total = upstream + summed_grad
        padded_grad = jnp.pad(upstream_total, ((half_width, half_width), (0, 0)))
        frame_grads.append((upstream_total + conv_transpose(padded_grad, kernel, FRAMES)).astype(jnp.bfloat16))
        grad_kernel = grad_kernel + kernel_terms(padded, upstream_total, KW, FRAMES)
        grad_gain = grad_gain + gain_term
        grad_router = grad_router + router_term
    return (jnp.stack(outputs), jnp.stack(frame_grads), grad_kernel, grad_gain, grad_router, grad_in, grad_out)
```

```python
import jax
import jax.numpy as jnp
from jax import lax
from jax.sharding import Mesh
from jax.sharding import PartitionSpec as P

eps = 1e-06

SEQ = ("z", "y", "xl", "c")
GRP = ("z", "y")


def padded_2(shard, axis, size, width):
    length = shard.shape[0]
    up = [(i, (i + 1) % size) for i in range(size - 1)]
    down = [(j, i) for i, j in up]
    last = lax.slice_in_dim(shard, length - width, length, axis=0)
    initial = lax.slice_in_dim(shard, 0, width, axis=0)
    before = lax.ppermute(last, axis, up)
    after = lax.ppermute(initial, axis, down)
    return jnp.concatenate([before, shard, after], axis=0)


def conv_forward(padded, kernel, row_count):
    summed = jnp.zeros((row_count, padded.shape[1]), jnp.float32)
    for offset in range(kernel.shape[0]):
        summed = summed + kernel[offset].astype(jnp.float32) * padded[
            offset : offset + row_count
        ].astype(jnp.float32)
    return summed


def conv_transpose(padded, kernel, row_count):
    length = kernel.shape[0]
    summed = jnp.zeros((row_count, padded.shape[1]), jnp.float32)
    for offset in range(length):
        start = length - 1 - offset
        summed = summed + kernel[offset].astype(jnp.float32) * padded[start : start + row_count]
    return summed


def kernel_terms(padded, upstream, length, row_count):
    return jnp.stack(
        [
            jnp.sum(padded[offset : offset + row_count].astype(jnp.float32) * upstream, axis=0)
            for offset in range(length)
        ]
    )


def normalize(summed, norm_gain):
    square = jnp.mean(summed * summed, axis=-1, keepdims=True)
    return summed * lax.rsqrt(square + eps) * norm_gain


def slot_numbers(expert_ids, expert_count):
    onehot = (expert_ids[:, None] == jnp.arange(expert_count, dtype=jnp.int32)[None, :]).astype(
        jnp.int32
    )
    ranks = jnp.cumsum(onehot, axis=0) - onehot
    return jnp.sum(ranks * onehot, axis=1)


def gate_values(normed_b, router, first_ids, second_ids):
    logits = jnp.dot(normed_b, router, preferred_element_type=jnp.float32)
    columns = jnp.arange(router.shape[1], dtype=jnp.int32)[None, :]
    pick_diff = (first_ids[:, None] == columns).astype(jnp.float32) - (
        second_ids[:, None] == columns
    ).astype(jnp.float32)
    gate_one = jax.nn.sigmoid(jnp.sum(logits * pick_diff, axis=1))
    return (gate_one, 1.0 - gate_one, pick_diff)


def swish_parts(pre_act):
    squash = jax.nn.sigmoid(pre_act)
    return (pre_act * squash, squash * (1.0 + pre_act * (1.0 - squash)))


def gate_backward(upstream, out_one, out_two, gate_one, gate_two, pick_diff, normed_b, router):
    grad_gap = (
        (jnp.sum(upstream * out_one, axis=1) - jnp.sum(upstream * out_two, axis=1))
        * gate_one
        * gate_two
    )
    grad_logits = (grad_gap[:, None] * pick_diff).astype(jnp.bfloat16)
    router_term = jnp.dot(normed_b.T, grad_logits, preferred_element_type=jnp.float32)
    normed_term = jnp.dot(grad_logits, router.T, preferred_element_type=jnp.float32)
    return (router_term, normed_term)


def body(frames, kernel, norm_gain, router, experts, w_in, w_out, cotangent):
    inputs_dev = frames[0]
    row_count = inputs_dev.shape[0]
    width = inputs_dev.shape[1]
    length = kernel.shape[0]
    half_width = length // 2
    expert_count = router.shape[1]
    top_count = experts.shape[2]
    capacity = 2 * row_count * top_count // expert_count
    seq_size = lax.psum(1, SEQ)
    in_weights = w_in[0]
    out_weights = w_out[0]
    padded = padded_2(inputs_dev, SEQ, seq_size, half_width)
    summed = inputs_dev.astype(jnp.float32) + conv_forward(padded, kernel, row_count)
    normed_b = normalize(summed, norm_gain).astype(jnp.bfloat16)
    choice_ids = experts[0]
    gate_one, gate_two, pick_diff = gate_values(
        normed_b, router, choice_ids[:, 0], choice_ids[:, 1]
    )
    flat_ids = choice_ids.reshape(-1)
    slot_index = slot_numbers(flat_ids, expert_count)
    position = flat_ids * capacity + slot_index
    dispatch_table = (
        lax.broadcasted_iota(jnp.int32, (expert_count * capacity, flat_ids.shape[0]), 0)
        == position[None, :]
    ).astype(jnp.bfloat16)

    upstream = cotangent[0].astype(jnp.float32)
    repeated = jnp.repeat(normed_b, top_count, axis=0)
    grad_assigned = jnp.stack([gate_one[:, None] * upstream, gate_two[:, None] * upstream], axis=1)
    grad_values = grad_assigned.reshape(row_count * top_count, width).astype(jnp.bfloat16)
    both = jnp.concatenate([repeated, grad_values], axis=1)
    packed = jnp.dot(dispatch_table, both, preferred_element_type=jnp.float32).astype(jnp.bfloat16)
    packed = packed.reshape(expert_count, capacity, 2 * width)
    arrived = lax.all_to_all(packed, GRP, split_axis=0, concat_axis=0, tiled=True)
    arrived = lax.all_gather(arrived, "xl", axis=0, tiled=False)
    arrived = lax.all_gather(arrived, "c", axis=0, tiled=False)
    rows_shape = arrived.shape
    flat = arrived.reshape(-1, 2 * width)
    flat_rows = flat[:, :width]
    flat_grads = flat[:, width:]

    pre_act = jnp.dot(flat_rows, in_weights, preferred_element_type=jnp.float32)
    hidden_f, slope = swish_parts(pre_act)
    hidden = hidden_f.astype(jnp.bfloat16)
    partial_rows = jnp.dot(hidden, out_weights, preferred_element_type=jnp.float32).astype(
        jnp.bfloat16
    )
    grad_hidden = jnp.dot(flat_grads, out_weights.T, preferred_element_type=jnp.float32)
    grad_pre = (grad_hidden * slope).astype(jnp.bfloat16)
    out_term = jnp.dot(hidden.T, flat_grads, preferred_element_type=jnp.float32)
    in_term = jnp.dot(flat_rows.T, grad_pre, preferred_element_type=jnp.float32)
    grad_part = jnp.dot(grad_pre, in_weights.T, preferred_element_type=jnp.float32).astype(
        jnp.bfloat16
    )

    dp_pair = [(0, 1), (1, 0)]
    in_mine, out_mine = in_term.astype(jnp.bfloat16), out_term.astype(jnp.bfloat16)
    in_other = lax.ppermute(in_mine, "dp", dp_pair)
    out_other = lax.ppermute(out_mine, "dp", dp_pair)
    dp_first = lax.axis_index("dp") == 0
    in_a = jnp.where(dp_first, in_mine, in_other).astype(jnp.float32)
    in_b = jnp.where(dp_first, in_other, in_mine).astype(jnp.float32)
    out_a = jnp.where(dp_first, out_mine, out_other).astype(jnp.float32)
    out_b = jnp.where(dp_first, out_other, out_mine).astype(jnp.float32)
    grad_in = in_a + in_b
    grad_out = out_a + out_b

    back = jnp.concatenate([partial_rows, grad_part], axis=1).reshape(rows_shape)
    back = lax.psum_scatter(back, "c", scatter_dimension=0, tiled=True)
    back = lax.psum_scatter(back, "xl", scatter_dimension=1, tiled=True)
    back = back.reshape(expert_count, capacity, 2 * width)
    totals = lax.all_to_all(back, GRP, split_axis=0, concat_axis=0, tiled=True)
    totals = totals.reshape(expert_count * capacity, 2 * width)
    picked = jnp.take(totals, position, axis=0).astype(jnp.float32)
    picked = picked.reshape(row_count, top_count, 2 * width)
    out_one = picked[:, 0, :width]
    out_two = picked[:, 1, :width]
    normed_grads = picked[:, 0, width:] + picked[:, 1, width:]

    mixed = (summed + gate_one[:, None] * out_one + gate_two[:, None] * out_two).astype(
        jnp.bfloat16
    )
    router_term, normed_term = gate_backward(
        upstream, out_one, out_two, gate_one, gate_two, pick_diff, normed_b, router
    )
    pullback = jax.vjp(normalize, summed, norm_gain)[1]
    summed_grad, gain_term = pullback(normed_grads + normed_term)
    upstream_total = upstream + summed_grad
    padded_grad = padded_2(
        upstream_total.astype(jnp.bfloat16), SEQ, seq_size, half_width
    ).astype(upstream_total.dtype)
    grad_frames = (upstream_total + conv_transpose(padded_grad, kernel, row_count)).astype(
        jnp.bfloat16
    )
    kernel_term = kernel_terms(padded, upstream_total, length, row_count)
    small = jnp.concatenate([kernel_term, gain_term[None, :], router_term.T], axis=0)
    for axis in ("c", "xl", "y", "z", "dp"):
        small = lax.psum(small, axis)
    grad_kernel = small[:length]
    grad_gain = small[length]
    grad_router = small[length + 1 :].T
    return (
        mixed[None],
        grad_frames[None],
        grad_kernel,
        grad_gain,
        grad_router,
        grad_in[None],
        grad_out[None],
    )


def solution(mesh):
    split_mesh = Mesh(mesh.devices.reshape(8, 4, 2, 2, 2), SEQ + ("dp",))
    return jax.shard_map(
        body,
        mesh=split_mesh,
        in_specs=(
            P("dp", SEQ, None),
            P(),
            P(),
            P(),
            P("dp", SEQ, None),
            P(SEQ, None, None),
            P(SEQ, None, None),
            P("dp", SEQ, None),
        ),
        out_specs=(
            P("dp", SEQ, None),
            P("dp", SEQ, None),
            P(),
            P(),
            P(),
            P(SEQ, None, None),
            P(SEQ, None, None),
        ),
        check_vma=False,
    )
```

```python
import jax
import jax.numpy as jnp
from jax import lax
from jax.sharding import Mesh
from jax.sharding import PartitionSpec as P

eps = 1e-06

SEQ = ("z", "y", "xl", "c")
GRP = ("z", "y")


def padded_2(shard, axis, size, width):
    length = shard.shape[0]
    up = [(i, (i + 1) % size) for i in range(size - 1)]
    down = [(j, i) for i, j in up]
    last = lax.slice_in_dim(shard, length - width, length, axis=0)
    initial = lax.slice_in_dim(shard, 0, width, axis=0)
    before = lax.ppermute(last, axis, up)
    after = lax.ppermute(initial, axis, down)
    return jnp.concatenate([before, shard, after], axis=0)


def conv_forward(padded, kernel, row_count):
    summed = jnp.zeros((row_count, padded.shape[1]), jnp.float32)
    for offset in range(kernel.shape[0]):
        summed = summed + kernel[offset].astype(jnp.float32) * padded[
            offset : offset + row_count
        ].astype(jnp.float32)
    return summed


def conv_transpose(padded, kernel, row_count):
    length = kernel.shape[0]
    summed = jnp.zeros((row_count, padded.shape[1]), jnp.float32)
    for offset in range(length):
        start = length - 1 - offset
        summed = summed + kernel[offset].astype(jnp.float32) * padded[start : start + row_count]
    return summed


def kernel_terms(padded, upstream, length, row_count):
    return jnp.stack(
        [
            jnp.sum(padded[offset : offset + row_count].astype(jnp.float32) * upstream, axis=0)
            for offset in range(length)
        ]
    )


def normalize(summed, norm_gain):
    square = jnp.mean(summed * summed, axis=-1, keepdims=True)
    return summed * lax.rsqrt(square + eps) * norm_gain


def slot_numbers(expert_ids, expert_count):
    onehot = (expert_ids[:, None] == jnp.arange(expert_count, dtype=jnp.int32)[None, :]).astype(
        jnp.int32
    )
    ranks = jnp.cumsum(onehot, axis=0) - onehot
    return jnp.sum(ranks * onehot, axis=1)


def gate_values(normed_b, router, first_ids, second_ids):
    logits = jnp.dot(normed_b, router, preferred_element_type=jnp.float32)
    columns = jnp.arange(router.shape[1], dtype=jnp.int32)[None, :]
    pick_diff = (first_ids[:, None] == columns).astype(jnp.float32) - (
        second_ids[:, None] == columns
    ).astype(jnp.float32)
    gate_one = jax.nn.sigmoid(jnp.sum(logits * pick_diff, axis=1))
    return (gate_one, 1.0 - gate_one, pick_diff)


def swish_parts(pre_act):
    squash = jax.nn.sigmoid(pre_act)
    return (pre_act * squash, squash * (1.0 + pre_act * (1.0 - squash)))


def gate_backward(upstream, out_one, out_two, gate_one, gate_two, pick_diff, normed_b, router):
    grad_gap = (
        (jnp.sum(upstream * out_one, axis=1) - jnp.sum(upstream * out_two, axis=1))
        * gate_one
        * gate_two
    )
    grad_logits = (grad_gap[:, None] * pick_diff).astype(jnp.bfloat16)
    router_term = jnp.dot(normed_b.T, grad_logits, preferred_element_type=jnp.float32)
    normed_term = jnp.dot(grad_logits, router.T, preferred_element_type=jnp.float32)
    return (router_term, normed_term)


def body(frames, kernel, norm_gain, router, experts, w_in, w_out, cotangent):
    inputs_dev = frames[0]
    row_count = inputs_dev.shape[0]
    width = inputs_dev.shape[1]
    length = kernel.shape[0]
    half_width = length // 2
    expert_count = router.shape[1]
    top_count = experts.shape[2]
    capacity = 2 * row_count * top_count // expert_count
    seq_size = lax.psum(1, SEQ)
    in_weights = w_in[0]
    out_weights = w_out[0]
    padded = padded_2(inputs_dev, SEQ, seq_size, half_width)
    summed = inputs_dev.astype(jnp.float32) + conv_forward(padded, kernel, row_count)
    normed_b = normalize(summed, norm_gain).astype(jnp.bfloat16)
    choice_ids = experts[0]
    gate_one, gate_two, pick_diff = gate_values(
        normed_b, router, choice_ids[:, 0], choice_ids[:, 1]
    )
    flat_ids = choice_ids.reshape(-1)
    slot_index = slot_numbers(flat_ids, expert_count)
    position = flat_ids * capacity + slot_index
    dispatch_table = (
        lax.broadcasted_iota(jnp.int32, (expert_count * capacity, flat_ids.shape[0]), 0)
        == position[None, :]
    ).astype(jnp.bfloat16)

    upstream = cotangent[0].astype(jnp.float32)
    repeated = jnp.repeat(normed_b, top_count, axis=0)
    grad_assigned = jnp.stack([gate_one[:, None] * upstream, gate_two[:, None] * upstream], axis=1)
    grad_values = grad_assigned.reshape(row_count * top_count, width).astype(jnp.bfloat16)
    both = jnp.concatenate([repeated, grad_values], axis=1)
    packed = jnp.dot(dispatch_table, both, preferred_element_type=jnp.float32).astype(jnp.bfloat16)
    packed = packed.reshape(expert_count, capacity, 2 * width)
    arrived = lax.all_to_all(packed, GRP, split_axis=0, concat_axis=0, tiled=True)
    in_all = lax.all_gather(lax.all_gather(in_weights, "xl", axis=0), "c", axis=0)
    out_all = lax.all_gather(lax.all_gather(out_weights, "xl", axis=0), "c", axis=0)
    slices = in_all.shape[0] * in_all.shape[1]
    hid = in_weights.shape[1]
    in_all = in_all.reshape(slices, width, hid)
    out_all = out_all.reshape(slices, hid, width)
    flat = arrived.reshape(-1, 2 * width)
    flat_rows = flat[:, :width]
    flat_grads = flat[:, width:]
    n_rows = flat.shape[0]

    in_cat = jnp.transpose(in_all, (1, 0, 2)).reshape(width, slices * hid)
    out_cat = out_all.reshape(slices * hid, width)
    pre_act = jnp.dot(flat_rows, in_cat, preferred_element_type=jnp.float32)
    hidden_f, slope = swish_parts(pre_act)
    hidden = hidden_f.astype(jnp.bfloat16)
    hidden_s = hidden.reshape(n_rows, slices, hid)
    partial_rows = jnp.einsum(
        "rsh,shd->srd", hidden_s, out_all, preferred_element_type=jnp.float32
    ).astype(jnp.bfloat16)
    expert_rows = partial_rows[0].astype(jnp.float32)
    for member in range(1, slices):
        expert_rows = expert_rows + partial_rows[member].astype(jnp.float32)
    grad_hidden = jnp.dot(flat_grads, out_cat.T, preferred_element_type=jnp.float32)
    grad_pre = (grad_hidden * slope).astype(jnp.bfloat16)
    out_term = jnp.dot(hidden.T, flat_grads, preferred_element_type=jnp.float32)
    in_term = jnp.dot(flat_rows.T, grad_pre, preferred_element_type=jnp.float32)
    grad_parts = jnp.einsum(
        "rsh,sdh->srd", grad_pre.reshape(n_rows, slices, hid), in_all,
        preferred_element_type=jnp.float32,
    ).astype(jnp.bfloat16)
    grad_rows = grad_parts[0].astype(jnp.float32)
    for member in range(1, slices):
        grad_rows = grad_rows + grad_parts[member].astype(jnp.float32)

    in_term = jnp.transpose(in_term.reshape(width, slices, hid), (1, 0, 2))
    in_term = in_term.reshape(2, 2, width, hid).astype(jnp.bfloat16)
    out_term = out_term.reshape(2, 2, hid, width).astype(jnp.bfloat16)
    in_mine = lax.psum_scatter(
        lax.psum_scatter(in_term, "c", scatter_dimension=0, tiled=True), "xl", scatter_dimension=1, tiled=True
    ).reshape(width, hid)
    out_mine = lax.psum_scatter(
        lax.psum_scatter(out_term, "c", scatter_dimension=0, tiled=True), "xl", scatter_dimension=1, tiled=True
    ).reshape(hid, width)
    dp_pair = [(0, 1), (1, 0)]
    in_other = lax.ppermute(in_mine, "dp", dp_pair)
    out_other = lax.ppermute(out_mine, "dp", dp_pair)
    dp_first = lax.axis_index("dp") == 0
    in_a = jnp.where(dp_first, in_mine, in_other).astype(jnp.float32)
    in_b = jnp.where(dp_first, in_other, in_mine).astype(jnp.float32)
    out_a = jnp.where(dp_first, out_mine, out_other).astype(jnp.float32)
    out_b = jnp.where(dp_first, out_other, out_mine).astype(jnp.float32)
    grad_in = in_a + in_b
    grad_out = out_a + out_b

    back = jnp.concatenate([expert_rows, grad_rows], axis=1).astype(jnp.bfloat16)
    back = back.reshape(expert_count, capacity, 2 * width)
    totals = lax.all_to_all(back, GRP, split_axis=0, concat_axis=0, tiled=True)
    totals = totals.reshape(expert_count * capacity, 2 * width)
    picked = jnp.take(totals, position, axis=0).astype(jnp.float32)
    picked = picked.reshape(row_count, top_count, 2 * width)
    out_one = picked[:, 0, :width]
    out_two = picked[:, 1, :width]
    normed_grads = picked[:, 0, width:] + picked[:, 1, width:]

    mixed = (summed + gate_one[:, None] * out_one + gate_two[:, None] * out_two).astype(
        jnp.bfloat16
    )
    router_term, normed_term = gate_backward(
        upstream, out_one, out_two, gate_one, gate_two, pick_diff, normed_b, router
    )
    pullback = jax.vjp(normalize, summed, norm_gain)[1]
    summed_grad, gain_term = pullback(normed_grads + normed_term)
    upstream_total = upstream + summed_grad
    padded_grad = padded_2(
        upstream_total.astype(jnp.bfloat16), SEQ, seq_size, half_width
    ).astype(upstream_total.dtype)
    grad_frames = (upstream_total + conv_transpose(padded_grad, kernel, row_count)).astype(
        jnp.bfloat16
    )
    kernel_term = kernel_terms(padded, upstream_total, length, row_count)
    small = jnp.concatenate([kernel_term, gain_term[None, :], router_term.T], axis=0)
    for axis, size in (("c", 2), ("xl", 2), ("y", 4), ("z", 8), ("dp", 2)):
        bit = 1
        while bit < size:
            small = small + lax.ppermute(small, axis, [(i, i ^ bit) for i in range(size)])
            bit *= 2
    grad_kernel = small[:length]
    grad_gain = small[length]
    grad_router = small[length + 1 :].T
    return (
        mixed[None],
        grad_frames[None],
        grad_kernel,
        grad_gain,
        grad_router,
        grad_in[None],
        grad_out[None],
    )


def solution(mesh):
    split_mesh = Mesh(mesh.devices.reshape(8, 4, 2, 2, 2), SEQ + ("dp",))
    return jax.shard_map(
        body,
        mesh=split_mesh,
        in_specs=(
            P("dp", SEQ, None),
            P(),
            P(),
            P(),
            P("dp", SEQ, None),
            P(SEQ, None, None),
            P(SEQ, None, None),
            P("dp", SEQ, None),
        ),
        out_specs=(
            P("dp", SEQ, None),
            P("dp", SEQ, None),
            P(),
            P(),
            P(),
            P(SEQ, None, None),
            P(SEQ, None, None),
        ),
        check_vma=False,
    )
```

```python
import jax
import jax.numpy as jnp
from jax import lax
from jax.sharding import Mesh
from jax.sharding import PartitionSpec as P

eps = 1e-06

SEQ = ("z", "y", "xl", "c")
GRP = ("z", "y")


def padded_2(shard, axis, size, width):
    length = shard.shape[0]
    up = [(i, (i + 1) % size) for i in range(size - 1)]
    down = [(j, i) for i, j in up]
    last = lax.slice_in_dim(shard, length - width, length, axis=0)
    initial = lax.slice_in_dim(shard, 0, width, axis=0)
    before = lax.ppermute(last, axis, up)
    after = lax.ppermute(initial, axis, down)
    return jnp.concatenate([before, shard, after], axis=0)


def swap(value, axis):
    return lax.ppermute(value, axis, [(0, 1), (1, 0)])


def gather_slices(weights):
    other_x = swap(weights, "xl")
    first_x = lax.axis_index("xl") == 0
    pair = jnp.where(first_x, jnp.stack([weights, other_x]), jnp.stack([other_x, weights]))
    other_c = swap(pair, "c")
    first_c = lax.axis_index("c") == 0
    return jnp.where(first_c, jnp.stack([pair, other_c]), jnp.stack([other_c, pair]))


def group_sum(value, axes, size):
    received = [value] + [
        lax.ppermute(value, axes, [(i, i ^ offset) for i in range(size)]) for offset in range(1, size)
    ]
    me = lax.axis_index(axes)
    stacked = jnp.stack(received)
    ordered = jnp.take(stacked, jnp.bitwise_xor(me, jnp.arange(size, dtype=me.dtype)), axis=0)
    total = ordered[0]
    for member in range(1, size):
        total = total + ordered[member]
    return total


def conv_forward(padded, kernel, row_count):
    summed = jnp.zeros((row_count, padded.shape[1]), jnp.float32)
    for offset in range(kernel.shape[0]):
        summed = summed + kernel[offset].astype(jnp.float32) * padded[
            offset : offset + row_count
        ].astype(jnp.float32)
    return summed


def conv_transpose(padded, kernel, row_count):
    length = kernel.shape[0]
    summed = jnp.zeros((row_count, padded.shape[1]), jnp.float32)
    for offset in range(length):
        start = length - 1 - offset
        summed = summed + kernel[offset].astype(jnp.float32) * padded[start : start + row_count]
    return summed


def kernel_terms(padded, upstream, length, row_count):
    return jnp.stack(
        [
            jnp.sum(padded[offset : offset + row_count].astype(jnp.float32) * upstream, axis=0)
            for offset in range(length)
        ]
    )


def normalize(summed, norm_gain):
    square = jnp.mean(summed * summed, axis=-1, keepdims=True)
    return summed * lax.rsqrt(square + eps) * norm_gain


def slot_numbers(expert_ids, expert_count):
    onehot = (expert_ids[:, None] == jnp.arange(expert_count, dtype=jnp.int32)[None, :]).astype(
        jnp.int32
    )
    ranks = jnp.cumsum(onehot, axis=0) - onehot
    return jnp.sum(ranks * onehot, axis=1)


def gate_values(normed_b, router, first_ids, second_ids):
    logits = jnp.dot(normed_b, router, preferred_element_type=jnp.float32)
    columns = jnp.arange(router.shape[1], dtype=jnp.int32)[None, :]
    pick_diff = (first_ids[:, None] == columns).astype(jnp.float32) - (
        second_ids[:, None] == columns
    ).astype(jnp.float32)
    gate_one = jax.nn.sigmoid(jnp.sum(logits * pick_diff, axis=1))
    return (gate_one, 1.0 - gate_one, pick_diff)


def swish_parts(pre_act):
    squash = jax.nn.sigmoid(pre_act)
    return (pre_act * squash, squash * (1.0 + pre_act * (1.0 - squash)))


def gate_backward(upstream, out_one, out_two, gate_one, gate_two, pick_diff, normed_b, router):
    grad_gap = (
        (jnp.sum(upstream * out_one, axis=1) - jnp.sum(upstream * out_two, axis=1))
        * gate_one
        * gate_two
    )
    grad_logits = (grad_gap[:, None] * pick_diff).astype(jnp.bfloat16)
    router_term = jnp.dot(normed_b.T, grad_logits, preferred_element_type=jnp.float32)
    normed_term = jnp.dot(grad_logits, router.T, preferred_element_type=jnp.float32)
    return (router_term, normed_term)


def body(frames, kernel, norm_gain, router, experts, w_in, w_out, cotangent):
    inputs_dev = frames[0]
    row_count = inputs_dev.shape[0]
    width = inputs_dev.shape[1]
    length = kernel.shape[0]
    half_width = length // 2
    expert_count = router.shape[1]
    top_count = experts.shape[2]
    capacity = 2 * row_count * top_count // expert_count
    seq_size = lax.psum(1, SEQ)
    in_weights = w_in[0]
    out_weights = w_out[0]
    padded = padded_2(inputs_dev, SEQ, seq_size, half_width)
    summed = inputs_dev.astype(jnp.float32) + conv_forward(padded, kernel, row_count)
    normed_b = normalize(summed, norm_gain).astype(jnp.bfloat16)
    choice_ids = experts[0]
    gate_one, gate_two, pick_diff = gate_values(
        normed_b, router, choice_ids[:, 0], choice_ids[:, 1]
    )
    flat_ids = choice_ids.reshape(-1)
    slot_index = slot_numbers(flat_ids, expert_count)
    position = flat_ids * capacity + slot_index
    dispatch_table = (
        lax.broadcasted_iota(jnp.int32, (expert_count * capacity, flat_ids.shape[0]), 0)
        == position[None, :]
    ).astype(jnp.bfloat16)

    upstream = cotangent[0].astype(jnp.float32)
    repeated = jnp.repeat(normed_b, top_count, axis=0)
    grad_assigned = jnp.stack([gate_one[:, None] * upstream, gate_two[:, None] * upstream], axis=1)
    grad_values = grad_assigned.reshape(row_count * top_count, width).astype(jnp.bfloat16)
    both = jnp.concatenate([repeated, grad_values], axis=1)
    packed = jnp.dot(dispatch_table, both, preferred_element_type=jnp.float32).astype(jnp.bfloat16)
    packed = packed.reshape(expert_count, capacity, 2 * width)
    arrived = lax.all_to_all(packed, GRP, split_axis=0, concat_axis=0, tiled=True)
    in_all = gather_slices(in_weights)
    out_all = gather_slices(out_weights)
    slices = in_all.shape[0] * in_all.shape[1]
    hid = in_weights.shape[1]
    in_all = in_all.reshape(slices, width, hid)
    out_all = out_all.reshape(slices, hid, width)
    flat = arrived.reshape(-1, 2 * width)
    flat_rows = flat[:, :width]
    flat_grads = flat[:, width:]
    n_rows = flat.shape[0]

    in_cat = jnp.transpose(in_all, (1, 0, 2)).reshape(width, slices * hid)
    out_cat = out_all.reshape(slices * hid, width)
    pre_act = jnp.dot(flat_rows, in_cat, preferred_element_type=jnp.float32)
    hidden_f, slope = swish_parts(pre_act)
    hidden = hidden_f.astype(jnp.bfloat16)
    hidden_s = hidden.reshape(n_rows, slices, hid)
    partial_rows = jnp.einsum(
        "rsh,shd->srd", hidden_s, out_all, preferred_element_type=jnp.float32
    ).astype(jnp.bfloat16)
    expert_rows = partial_rows[0].astype(jnp.float32)
    for member in range(1, slices):
        expert_rows = expert_rows + partial_rows[member].astype(jnp.float32)
    grad_hidden = jnp.dot(flat_grads, out_cat.T, preferred_element_type=jnp.float32)
    grad_pre = (grad_hidden * slope).astype(jnp.bfloat16)
    out_term = jnp.dot(hidden.T, flat_grads, preferred_element_type=jnp.float32)
    in_term = jnp.dot(flat_rows.T, grad_pre, preferred_element_type=jnp.float32)
    grad_parts = jnp.einsum(
        "rsh,sdh->srd", grad_pre.reshape(n_rows, slices, hid), in_all,
        preferred_element_type=jnp.float32,
    ).astype(jnp.bfloat16)
    grad_rows = grad_parts[0].astype(jnp.float32)
    for member in range(1, slices):
        grad_rows = grad_rows + grad_parts[member].astype(jnp.float32)

    in_term = jnp.transpose(in_term.reshape(width, slices, hid), (1, 0, 2))
    in_term = in_term.reshape(2, 2, width, hid)
    out_term = out_term.reshape(2, 2, width, hid)
    terms = jnp.concatenate([in_term, out_term], axis=3).astype(jnp.bfloat16)
    terms = lax.psum_scatter(terms, "c", scatter_dimension=0, tiled=True)
    terms = lax.psum_scatter(terms, "xl", scatter_dimension=1, tiled=True).reshape(width, 2 * hid)
    in_mine = terms[:, :hid]
    out_mine = terms[:, hid:].reshape(hid, width)
    dp_pair = [(0, 1), (1, 0)]
    in_other = lax.ppermute(in_mine, "dp", dp_pair)
    out_other = lax.ppermute(out_mine, "dp", dp_pair)
    dp_first = lax.axis_index("dp") == 0
    in_a = jnp.where(dp_first, in_mine, in_other).astype(jnp.float32)
    in_b = jnp.where(dp_first, in_other, in_mine).astype(jnp.float32)
    out_a = jnp.where(dp_first, out_mine, out_other).astype(jnp.float32)
    out_b = jnp.where(dp_first, out_other, out_mine).astype(jnp.float32)
    grad_in = in_a + in_b
    grad_out = out_a + out_b

    back = jnp.concatenate([expert_rows, grad_rows], axis=1).astype(jnp.bfloat16)
    back = back.reshape(expert_count, capacity, 2 * width)
    totals = lax.all_to_all(back, GRP, split_axis=0, concat_axis=0, tiled=True)
    totals = totals.reshape(expert_count * capacity, 2 * width)
    picked = jnp.take(totals, position, axis=0).astype(jnp.float32)
    picked = picked.reshape(row_count, top_count, 2 * width)
    out_one = picked[:, 0, :width]
    out_two = picked[:, 1, :width]
    normed_grads = picked[:, 0, width:] + picked[:, 1, width:]

    mixed = (summed + gate_one[:, None] * out_one + gate_two[:, None] * out_two).astype(
        jnp.bfloat16
    )
    router_term, normed_term = gate_backward(
        upstream, out_one, out_two, gate_one, gate_two, pick_diff, normed_b, router
    )
    pullback = jax.vjp(normalize, summed, norm_gain)[1]
    summed_grad, gain_term = pullback(normed_grads + normed_term)
    upstream_total = upstream + summed_grad
    padded_grad = padded_2(
        upstream_total.astype(jnp.bfloat16), SEQ, seq_size, half_width
    ).astype(upstream_total.dtype)
    grad_frames = (upstream_total + conv_transpose(padded_grad, kernel, row_count)).astype(
        jnp.bfloat16
    )
    kernel_term = kernel_terms(padded, upstream_total, length, row_count)
    small = jnp.concatenate([kernel_term, gain_term[None, :], router_term.T], axis=0)
    small = group_sum(small, ("xl", "c", "dp"), 8)
    small = group_sum(small, "y", 4)
    for bit in (1, 2, 4):
        small = small + lax.ppermute(small, "z", [(i, i ^ bit) for i in range(8)])
    grad_kernel = small[:length]
    grad_gain = small[length]
    grad_router = small[length + 1 :].T
    return (
        mixed[None],
        grad_frames[None],
        grad_kernel,
        grad_gain,
        grad_router,
        grad_in[None],
        grad_out[None],
    )


def solution(mesh):
    split_mesh = Mesh(mesh.devices.reshape(8, 4, 2, 2, 2), SEQ + ("dp",))
    return jax.shard_map(
        body,
        mesh=split_mesh,
        in_specs=(
            P("dp", SEQ, None),
            P(),
            P(),
            P(),
            P("dp", SEQ, None),
            P(SEQ, None, None),
            P(SEQ, None, None),
            P("dp", SEQ, None),
        ),
        out_specs=(
            P("dp", SEQ, None),
            P("dp", SEQ, None),
            P(),
            P(),
            P(),
            P(SEQ, None, None),
            P(SEQ, None, None),
        ),
        check_vma=False,
    )
```

```python
import jax
import jax.numpy as jnp
from jax import lax
from jax.sharding import Mesh
from jax.sharding import PartitionSpec as P

eps = 1e-06

SEQ = ("z", "y", "xl", "c")
GRP = ("z", "y")


def padded_2(shard, axis, size, width):
    length = shard.shape[0]
    up = [(i, (i + 1) % size) for i in range(size - 1)]
    down = [(j, i) for i, j in up]
    last = lax.slice_in_dim(shard, length - width, length, axis=0)
    initial = lax.slice_in_dim(shard, 0, width, axis=0)
    before = lax.ppermute(last, axis, up)
    after = lax.ppermute(initial, axis, down)
    return jnp.concatenate([before, shard, after], axis=0)


def swap(value, axis):
    return lax.ppermute(value, axis, [(0, 1), (1, 0)])


def gather_slices(weights):
    pair = jnp.stack([weights, swap(weights, "xl")])
    return jnp.stack([pair, swap(pair, "c")])


def group_sum(value, axes, size):
    received = [value] + [
        lax.ppermute(value, axes, [(i, i ^ offset) for i in range(size)]) for offset in range(1, size)
    ]
    me = lax.axis_index(axes)
    stacked = jnp.stack(received)
    ordered = jnp.take(stacked, jnp.bitwise_xor(me, jnp.arange(size, dtype=me.dtype)), axis=0)
    total = ordered[0]
    for member in range(1, size):
        total = total + ordered[member]
    return total


def conv_forward(padded, kernel, row_count):
    summed = jnp.zeros((row_count, padded.shape[1]), jnp.float32)
    for offset in range(kernel.shape[0]):
        summed = summed + kernel[offset].astype(jnp.float32) * padded[
            offset : offset + row_count
        ].astype(jnp.float32)
    return summed


def conv_transpose(padded, kernel, row_count):
    length = kernel.shape[0]
    summed = jnp.zeros((row_count, padded.shape[1]), jnp.float32)
    for offset in range(length):
        start = length - 1 - offset
        summed = summed + kernel[offset].astype(jnp.float32) * padded[start : start + row_count]
    return summed


def kernel_terms(padded, upstream, length, row_count):
    return jnp.stack(
        [
            jnp.sum(padded[offset : offset + row_count].astype(jnp.float32) * upstream, axis=0)
            for offset in range(length)
        ]
    )


def normalize(summed, norm_gain):
    square = jnp.mean(summed * summed, axis=-1, keepdims=True)
    return summed * lax.rsqrt(square + eps) * norm_gain


def slot_numbers(expert_ids, expert_count):
    onehot = (expert_ids[:, None] == jnp.arange(expert_count, dtype=jnp.int32)[None, :]).astype(
        jnp.int32
    )
    ranks = jnp.cumsum(onehot, axis=0) - onehot
    return jnp.sum(ranks * onehot, axis=1)


def gate_values(normed_b, router, first_ids, second_ids):
    logits = jnp.dot(normed_b, router, preferred_element_type=jnp.float32)
    columns = jnp.arange(router.shape[1], dtype=jnp.int32)[None, :]
    pick_diff = (first_ids[:, None] == columns).astype(jnp.float32) - (
        second_ids[:, None] == columns
    ).astype(jnp.float32)
    gate_one = jax.nn.sigmoid(jnp.sum(logits * pick_diff, axis=1))
    return (gate_one, 1.0 - gate_one, pick_diff)


def swish_parts(pre_act):
    squash = jax.nn.sigmoid(pre_act)
    return (pre_act * squash, squash * (1.0 + pre_act * (1.0 - squash)))


def gate_backward(upstream, out_one, out_two, gate_one, gate_two, pick_diff, normed_b, router):
    grad_gap = (
        (jnp.sum(upstream * out_one, axis=1) - jnp.sum(upstream * out_two, axis=1))
        * gate_one
        * gate_two
    )
    grad_logits = (grad_gap[:, None] * pick_diff).astype(jnp.bfloat16)
    router_term = jnp.dot(normed_b.T, grad_logits, preferred_element_type=jnp.float32)
    normed_term = jnp.dot(grad_logits, router.T, preferred_element_type=jnp.float32)
    return (router_term, normed_term)


def body(frames, kernel, norm_gain, router, experts, w_in, w_out, cotangent):
    inputs_dev = frames[0]
    row_count = inputs_dev.shape[0]
    width = inputs_dev.shape[1]
    length = kernel.shape[0]
    half_width = length // 2
    expert_count = router.shape[1]
    top_count = experts.shape[2]
    capacity = 2 * row_count * top_count // expert_count
    seq_size = lax.psum(1, SEQ)
    in_weights = w_in[0]
    out_weights = w_out[0]
    padded = padded_2(inputs_dev, SEQ, seq_size, half_width)
    summed = inputs_dev.astype(jnp.float32) + conv_forward(padded, kernel, row_count)
    normed_b = normalize(summed, norm_gain).astype(jnp.bfloat16)
    choice_ids = experts[0]
    gate_one, gate_two, pick_diff = gate_values(
        normed_b, router, choice_ids[:, 0], choice_ids[:, 1]
    )
    flat_ids = choice_ids.reshape(-1)
    slot_index = slot_numbers(flat_ids, expert_count)
    position = flat_ids * capacity + slot_index
    dispatch_table = (
        lax.broadcasted_iota(jnp.int32, (expert_count * capacity, flat_ids.shape[0]), 0)
        == position[None, :]
    ).astype(jnp.bfloat16)

    upstream = cotangent[0].astype(jnp.float32)
    repeated = jnp.repeat(normed_b, top_count, axis=0)
    grad_assigned = jnp.stack([gate_one[:, None] * upstream, gate_two[:, None] * upstream], axis=1)
    grad_values = grad_assigned.reshape(row_count * top_count, width).astype(jnp.bfloat16)
    both = jnp.concatenate([repeated, grad_values], axis=1)
    packed = jnp.dot(dispatch_table, both, preferred_element_type=jnp.float32).astype(jnp.bfloat16)
    packed = packed.reshape(expert_count, capacity, 2 * width)
    arrived = lax.all_to_all(packed, GRP, split_axis=0, concat_axis=0, tiled=True)
    in_all = gather_slices(in_weights)
    out_all = gather_slices(out_weights)
    slices = in_all.shape[0] * in_all.shape[1]
    hid = in_weights.shape[1]
    in_all = in_all.reshape(slices, width, hid)
    out_all = out_all.reshape(slices, hid, width)
    flat = arrived.reshape(-1, 2 * width)
    flat_rows = flat[:, :width]
    flat_grads = flat[:, width:]
    n_rows = flat.shape[0]

    in_cat = jnp.transpose(in_all, (1, 0, 2)).reshape(width, slices * hid)
    out_cat = out_all.reshape(slices * hid, width)
    pre_act = jnp.dot(flat_rows, in_cat, preferred_element_type=jnp.float32)
    hidden_f, slope = swish_parts(pre_act)
    hidden = hidden_f.astype(jnp.bfloat16)
    hidden_s = hidden.reshape(n_rows, slices, hid)
    partial_rows = jnp.einsum(
        "rsh,shd->srd", hidden_s, out_all, preferred_element_type=jnp.float32
    ).astype(jnp.bfloat16)
    expert_rows = partial_rows[0].astype(jnp.float32)
    for member in range(1, slices):
        expert_rows = expert_rows + partial_rows[member].astype(jnp.float32)
    grad_hidden = jnp.dot(flat_grads, out_cat.T, preferred_element_type=jnp.float32)
    grad_pre = (grad_hidden * slope).astype(jnp.bfloat16)
    out_term = jnp.dot(hidden.T, flat_grads, preferred_element_type=jnp.float32)
    in_term = jnp.dot(flat_rows.T, grad_pre, preferred_element_type=jnp.float32)
    grad_parts = jnp.einsum(
        "rsh,sdh->srd", grad_pre.reshape(n_rows, slices, hid), in_all,
        preferred_element_type=jnp.float32,
    ).astype(jnp.bfloat16)
    grad_rows = grad_parts[0].astype(jnp.float32)
    for member in range(1, slices):
        grad_rows = grad_rows + grad_parts[member].astype(jnp.float32)

    in_term = jnp.transpose(in_term.reshape(width, slices, hid), (1, 0, 2))
    in_term = in_term.reshape(2, 2, width, hid)
    out_term = out_term.reshape(2, 2, width, hid)
    terms = jnp.concatenate([in_term, out_term], axis=3).astype(jnp.bfloat16)
    pair_terms = terms[0].astype(jnp.float32) + swap(terms[1], "c").astype(jnp.float32)
    own_terms = pair_terms[0] + swap(pair_terms[1].astype(jnp.bfloat16), "xl").astype(jnp.float32)
    mine = own_terms.astype(jnp.bfloat16)
    other = swap(mine, "dp")
    dp_first = lax.axis_index("dp") == 0
    first = jnp.where(dp_first, mine, other).astype(jnp.float32)
    second = jnp.where(dp_first, other, mine).astype(jnp.float32)
    grad_terms = first + second
    grad_in = grad_terms[:, :hid]
    grad_out = grad_terms[:, hid:].reshape(hid, width)

    back = jnp.concatenate([expert_rows, grad_rows], axis=1).astype(jnp.bfloat16)
    back = back.reshape(expert_count, capacity, 2 * width)
    totals = lax.all_to_all(back, GRP, split_axis=0, concat_axis=0, tiled=True)
    totals = totals.reshape(expert_count * capacity, 2 * width)
    picked = jnp.take(totals, position, axis=0).astype(jnp.float32)
    picked = picked.reshape(row_count, top_count, 2 * width)
    out_one = picked[:, 0, :width]
    out_two = picked[:, 1, :width]
    normed_grads = picked[:, 0, width:] + picked[:, 1, width:]

    mixed = (summed + gate_one[:, None] * out_one + gate_two[:, None] * out_two).astype(
        jnp.bfloat16
    )
    router_term, normed_term = gate_backward(
        upstream, out_one, out_two, gate_one, gate_two, pick_diff, normed_b, router
    )
    pullback = jax.vjp(normalize, summed, norm_gain)[1]
    summed_grad, gain_term = pullback(normed_grads + normed_term)
    upstream_total = upstream + summed_grad
    padded_grad = padded_2(
        upstream_total.astype(jnp.bfloat16), SEQ, seq_size, half_width
    ).astype(upstream_total.dtype)
    grad_frames = (upstream_total + conv_transpose(padded_grad, kernel, row_count)).astype(
        jnp.bfloat16
    )
    kernel_term = kernel_terms(padded, upstream_total, length, row_count)
    small = jnp.concatenate([kernel_term, gain_term[None, :], router_term.T], axis=0)
    local = ("xl", "c", "dp")
    chunks = small.reshape(8, small.shape[0] // 8, small.shape[1])
    me = lax.axis_index(local)
    chunk = lax.dynamic_index_in_dim(chunks, me, axis=0, keepdims=False)
    for offset in range(1, 8):
        piece = lax.dynamic_index_in_dim(chunks, jnp.bitwise_xor(me, offset), axis=0, keepdims=False)
        chunk = chunk + lax.ppermute(piece, local, [(i, i ^ offset) for i in range(8)])
    chunk = group_sum(chunk, "y", 4)
    for bit in (1, 2, 4):
        chunk = chunk + lax.ppermute(chunk, "z", [(i, i ^ bit) for i in range(8)])
    gathered = [chunk] + [
        lax.ppermute(chunk, local, [(i, i ^ offset) for i in range(8)]) for offset in range(1, 8)
    ]
    small = jnp.take(jnp.stack(gathered), jnp.bitwise_xor(me, jnp.arange(8, dtype=me.dtype)), axis=0)
    small = small.reshape(chunks.shape[0] * chunks.shape[1], chunks.shape[2])
    grad_kernel = small[:length]
    grad_gain = small[length]
    grad_router = small[length + 1 :].T
    return (
        mixed[None],
        grad_frames[None],
        grad_kernel,
        grad_gain,
        grad_router,
        grad_in[None],
        grad_out[None],
    )


def solution(mesh):
    split_mesh = Mesh(mesh.devices.reshape(8, 4, 2, 2, 2), SEQ + ("dp",))
    return jax.shard_map(
        body,
        mesh=split_mesh,
        in_specs=(
            P("dp", SEQ, None),
            P(),
            P(),
            P(),
            P("dp", SEQ, None),
            P(SEQ, None, None),
            P(SEQ, None, None),
            P("dp", SEQ, None),
        ),
        out_specs=(
            P("dp", SEQ, None),
            P("dp", SEQ, None),
            P(),
            P(),
            P(),
            P(SEQ, None, None),
            P(SEQ, None, None),
        ),
        check_vma=False,
    )
```

```python
import jax
import jax.numpy as jnp
from jax import lax
from jax.sharding import Mesh
from jax.sharding import PartitionSpec as P

eps = 1e-06

SEQ = ("z", "y", "xl", "c")
GRP = ("z", "y")


def padded_2(shard, axis, size, width):
    length = shard.shape[0]
    up = [(i, (i + 1) % size) for i in range(size - 1)]
    down = [(j, i) for i, j in up]
    last = lax.slice_in_dim(shard, length - width, length, axis=0)
    initial = lax.slice_in_dim(shard, 0, width, axis=0)
    before = lax.ppermute(last, axis, up)
    after = lax.ppermute(initial, axis, down)
    return jnp.concatenate([before, shard, after], axis=0)


def swap(value, axis):
    return lax.ppermute(value, axis, [(0, 1), (1, 0)])


def gather_slices(weights):
    pair = jnp.stack([weights, swap(weights, "xl")])
    return jnp.stack([pair, swap(pair, "c")])


def group_sum(value, axes, size):
    received = [value] + [
        lax.ppermute(value, axes, [(i, i ^ offset) for i in range(size)]) for offset in range(1, size)
    ]
    me = lax.axis_index(axes)
    stacked = jnp.stack(received)
    ordered = jnp.take(stacked, jnp.bitwise_xor(me, jnp.arange(size, dtype=me.dtype)), axis=0)
    total = ordered[0]
    for member in range(1, size):
        total = total + ordered[member]
    return total


def conv_forward(padded, kernel, row_count):
    summed = jnp.zeros((row_count, padded.shape[1]), jnp.float32)
    for offset in range(kernel.shape[0]):
        summed = summed + kernel[offset].astype(jnp.float32) * padded[
            offset : offset + row_count
        ].astype(jnp.float32)
    return summed


def conv_transpose(padded, kernel, row_count):
    length = kernel.shape[0]
    summed = jnp.zeros((row_count, padded.shape[1]), jnp.float32)
    for offset in range(length):
        start = length - 1 - offset
        summed = summed + kernel[offset].astype(jnp.float32) * padded[start : start + row_count]
    return summed


def kernel_terms(padded, upstream, length, row_count):
    return jnp.stack(
        [
            jnp.sum(padded[offset : offset + row_count].astype(jnp.float32) * upstream, axis=0)
            for offset in range(length)
        ]
    )


def normalize(summed, norm_gain):
    square = jnp.mean(summed * summed, axis=-1, keepdims=True)
    return summed * lax.rsqrt(square + eps) * norm_gain


def slot_numbers(expert_ids, expert_count):
    onehot = (expert_ids[:, None] == jnp.arange(expert_count, dtype=jnp.int32)[None, :]).astype(
        jnp.int32
    )
    ranks = jnp.cumsum(onehot, axis=0) - onehot
    return jnp.sum(ranks * onehot, axis=1)


def gate_values(normed_b, router, first_ids, second_ids):
    logits = jnp.dot(normed_b, router, preferred_element_type=jnp.float32)
    columns = jnp.arange(router.shape[1], dtype=jnp.int32)[None, :]
    pick_diff = (first_ids[:, None] == columns).astype(jnp.float32) - (
        second_ids[:, None] == columns
    ).astype(jnp.float32)
    gate_one = jax.nn.sigmoid(jnp.sum(logits * pick_diff, axis=1))
    return (gate_one, 1.0 - gate_one, pick_diff)


def swish_parts(pre_act):
    squash = jax.nn.sigmoid(pre_act)
    return (pre_act * squash, squash * (1.0 + pre_act * (1.0 - squash)))


def gate_backward(upstream, out_one, out_two, gate_one, gate_two, pick_diff, normed_b, router):
    grad_gap = (
        (jnp.sum(upstream * out_one, axis=1) - jnp.sum(upstream * out_two, axis=1))
        * gate_one
        * gate_two
    )
    grad_logits = (grad_gap[:, None] * pick_diff).astype(jnp.bfloat16)
    router_term = jnp.dot(normed_b.T, grad_logits, preferred_element_type=jnp.float32)
    normed_term = jnp.dot(grad_logits, router.T, preferred_element_type=jnp.float32)
    return (router_term, normed_term)


def body(frames, kernel, norm_gain, router, experts, w_in, w_out, cotangent):
    inputs_dev = frames[0]
    row_count = inputs_dev.shape[0]
    width = inputs_dev.shape[1]
    length = kernel.shape[0]
    half_width = length // 2
    expert_count = router.shape[1]
    top_count = experts.shape[2]
    capacity = 2 * row_count * top_count // expert_count
    seq_size = lax.psum(1, SEQ)
    in_weights = w_in[0]
    out_weights = w_out[0]
    padded = padded_2(inputs_dev, SEQ, seq_size, half_width)
    summed = inputs_dev.astype(jnp.float32) + conv_forward(padded, kernel, row_count)
    normed_b = normalize(summed, norm_gain).astype(jnp.bfloat16)
    choice_ids = experts[0]
    gate_one, gate_two, pick_diff = gate_values(
        normed_b, router, choice_ids[:, 0], choice_ids[:, 1]
    )
    flat_ids = choice_ids.reshape(-1)
    slot_index = slot_numbers(flat_ids, expert_count)
    position = flat_ids * capacity + slot_index
    dispatch_table = (
        lax.broadcasted_iota(jnp.int32, (expert_count * capacity, flat_ids.shape[0]), 0)
        == position[None, :]
    ).astype(jnp.bfloat16)

    upstream = cotangent[0].astype(jnp.float32)
    repeated = jnp.repeat(normed_b, top_count, axis=0)
    grad_assigned = jnp.stack([gate_one[:, None] * upstream, gate_two[:, None] * upstream], axis=1)
    grad_values = grad_assigned.reshape(row_count * top_count, width).astype(jnp.bfloat16)
    both = jnp.concatenate([repeated, grad_values], axis=1)
    packed = jnp.dot(dispatch_table, both, preferred_element_type=jnp.float32).astype(jnp.bfloat16)
    packed = packed.reshape(expert_count, capacity, 2 * width)
    arrived = lax.all_to_all(packed, GRP, split_axis=0, concat_axis=0, tiled=True)
    hid = in_weights.shape[1]
    both_weights = gather_slices(jnp.stack([in_weights, out_weights.reshape(width, hid)]))
    in_all = both_weights[:, :, 0]
    out_all = both_weights[:, :, 1]
    slices = in_all.shape[0] * in_all.shape[1]
    in_all = in_all.reshape(slices, width, hid)
    out_all = out_all.reshape(slices, hid, width)
    flat = arrived.reshape(-1, 2 * width)
    flat_rows = flat[:, :width]
    flat_grads = flat[:, width:]
    n_rows = flat.shape[0]

    in_cat = jnp.transpose(in_all, (1, 0, 2)).reshape(width, slices * hid)
    out_cat = out_all.reshape(slices * hid, width)
    pre_act = jnp.dot(flat_rows, in_cat, preferred_element_type=jnp.float32)
    hidden_f, slope = swish_parts(pre_act)
    hidden = hidden_f.astype(jnp.bfloat16)
    hidden_s = hidden.reshape(n_rows, slices, hid)
    partial_rows = jnp.einsum(
        "rsh,shd->srd", hidden_s, out_all, preferred_element_type=jnp.float32
    ).astype(jnp.bfloat16)
    expert_rows = partial_rows[0].astype(jnp.float32)
    for member in range(1, slices):
        expert_rows = expert_rows + partial_rows[member].astype(jnp.float32)
    grad_hidden = jnp.dot(flat_grads, out_cat.T, preferred_element_type=jnp.float32)
    grad_pre = (grad_hidden * slope).astype(jnp.bfloat16)
    out_term = jnp.dot(hidden.T, flat_grads, preferred_element_type=jnp.float32)
    in_term = jnp.dot(flat_rows.T, grad_pre, preferred_element_type=jnp.float32)
    grad_parts = jnp.einsum(
        "rsh,sdh->srd", grad_pre.reshape(n_rows, slices, hid), in_all,
        preferred_element_type=jnp.float32,
    ).astype(jnp.bfloat16)
    grad_rows = grad_parts[0].astype(jnp.float32)
    for member in range(1, slices):
        grad_rows = grad_rows + grad_parts[member].astype(jnp.float32)

    in_term = jnp.transpose(in_term.reshape(width, slices, hid), (1, 0, 2))
    in_term = in_term.reshape(2, 2, width, hid)
    out_term = out_term.reshape(2, 2, width, hid)
    terms = jnp.concatenate([in_term, out_term], axis=3).astype(jnp.bfloat16)
    terms = jnp.where(lax.axis_index("c") == 0, terms, terms[::-1])
    terms = jnp.where(lax.axis_index("xl") == 0, terms, terms[:, ::-1])
    terms = lax.psum_scatter(terms, "c", scatter_dimension=0, tiled=True)
    terms = lax.psum_scatter(terms, "xl", scatter_dimension=1, tiled=True)
    own_terms = terms.reshape(width, 2 * hid)
    mine = own_terms.astype(jnp.bfloat16)
    other = swap(mine, "dp")
    dp_first = lax.axis_index("dp") == 0
    first = jnp.where(dp_first, mine, other).astype(jnp.float32)
    second = jnp.where(dp_first, other, mine).astype(jnp.float32)
    grad_terms = first + second
    grad_in = grad_terms[:, :hid]
    grad_out = grad_terms[:, hid:].reshape(hid, width)

    back = jnp.concatenate([expert_rows, grad_rows], axis=1).astype(jnp.bfloat16)
    back = back.reshape(expert_count, capacity, 2 * width)
    totals = lax.all_to_all(back, GRP, split_axis=0, concat_axis=0, tiled=True)
    totals = totals.reshape(expert_count * capacity, 2 * width)
    picked = jnp.take(totals, position, axis=0).astype(jnp.float32)
    picked = picked.reshape(row_count, top_count, 2 * width)
    out_one = picked[:, 0, :width]
    out_two = picked[:, 1, :width]
    normed_grads = picked[:, 0, width:] + picked[:, 1, width:]

    mixed = (summed + gate_one[:, None] * out_one + gate_two[:, None] * out_two).astype(
        jnp.bfloat16
    )
    router_term, normed_term = gate_backward(
        upstream, out_one, out_two, gate_one, gate_two, pick_diff, normed_b, router
    )
    pullback = jax.vjp(normalize, summed, norm_gain)[1]
    summed_grad, gain_term = pullback(normed_grads + normed_term)
    upstream_total = upstream + summed_grad
    padded_grad = padded_2(
        upstream_total.astype(jnp.bfloat16), SEQ, seq_size, half_width
    ).astype(upstream_total.dtype)
    grad_frames = (upstream_total + conv_transpose(padded_grad, kernel, row_count)).astype(
        jnp.bfloat16
    )
    kernel_term = kernel_terms(padded, upstream_total, length, row_count)
    small = jnp.concatenate([kernel_term, gain_term[None, :], router_term.T], axis=0)
    local = ("xl", "c", "dp")
    chunks = small.reshape(8, small.shape[0] // 8, small.shape[1])
    me = lax.axis_index(local)
    chunk = lax.dynamic_index_in_dim(chunks, me, axis=0, keepdims=False)
    for offset in range(1, 8):
        piece = lax.dynamic_index_in_dim(chunks, jnp.bitwise_xor(me, offset), axis=0, keepdims=False)
        chunk = chunk + lax.ppermute(piece, local, [(i, i ^ offset) for i in range(8)])
    chunk = group_sum(chunk, "y", 4)
    for bit in (1, 2, 4):
        chunk = chunk + lax.ppermute(chunk, "z", [(i, i ^ bit) for i in range(8)])
    gathered = [chunk] + [
        lax.ppermute(chunk, local, [(i, i ^ offset) for i in range(8)]) for offset in range(1, 8)
    ]
    small = jnp.take(jnp.stack(gathered), jnp.bitwise_xor(me, jnp.arange(8, dtype=me.dtype)), axis=0)
    small = small.reshape(chunks.shape[0] * chunks.shape[1], chunks.shape[2])
    grad_kernel = small[:length]
    grad_gain = small[length]
    grad_router = small[length + 1 :].T
    return (
        mixed[None],
        grad_frames[None],
        grad_kernel,
        grad_gain,
        grad_router,
        grad_in[None],
        grad_out[None],
    )


def solution(mesh):
    split_mesh = Mesh(mesh.devices.reshape(8, 4, 2, 2, 2), SEQ + ("dp",))
    return jax.shard_map(
        body,
        mesh=split_mesh,
        in_specs=(
            P("dp", SEQ, None),
            P(),
            P(),
            P(),
            P("dp", SEQ, None),
            P(SEQ, None, None),
            P(SEQ, None, None),
            P("dp", SEQ, None),
        ),
        out_specs=(
            P("dp", SEQ, None),
            P("dp", SEQ, None),
            P(),
            P(),
            P(),
            P(SEQ, None, None),
            P(SEQ, None, None),
        ),
        check_vma=False,
    )
```

```python
import jax
import jax.numpy as jnp
from jax import lax
from jax.sharding import Mesh
from jax.sharding import PartitionSpec as P

eps = 1e-06

SEQ = ("z", "y", "xl", "c")
GRP = ("z", "y")


def padded_2(shard, axis, size, width):
    length = shard.shape[0]
    up = [(i, (i + 1) % size) for i in range(size - 1)]
    down = [(j, i) for i, j in up]
    last = lax.slice_in_dim(shard, length - width, length, axis=0)
    initial = lax.slice_in_dim(shard, 0, width, axis=0)
    before = lax.ppermute(last, axis, up)
    after = lax.ppermute(initial, axis, down)
    return jnp.concatenate([before, shard, after], axis=0)


def swap(value, axis):
    return lax.ppermute(value, axis, [(0, 1), (1, 0)])


def gather_slices(weights):
    pair = jnp.stack([weights, swap(weights, "xl")])
    return jnp.stack([pair, swap(pair, "c")])


def group_sum(value, axes, size):
    received = [value] + [
        lax.ppermute(value, axes, [(i, i ^ offset) for i in range(size)]) for offset in range(1, size)
    ]
    me = lax.axis_index(axes)
    stacked = jnp.stack(received)
    ordered = jnp.take(stacked, jnp.bitwise_xor(me, jnp.arange(size, dtype=me.dtype)), axis=0)
    total = ordered[0]
    for member in range(1, size):
        total = total + ordered[member]
    return total


def reduce_scatter(value, axis, size):
    chunks = value.reshape(size, value.shape[0] // size, *value.shape[1:])
    me = lax.axis_index(axis)
    total = lax.dynamic_index_in_dim(chunks, me, axis=0, keepdims=False)
    for offset in range(1, size):
        piece = lax.dynamic_index_in_dim(chunks, jnp.bitwise_xor(me, offset), axis=0, keepdims=False)
        total = total + lax.ppermute(piece, axis, [(i, i ^ offset) for i in range(size)])
    return total


def all_gather(value, axis, size):
    me = lax.axis_index(axis)
    received = [value] + [
        lax.ppermute(value, axis, [(i, i ^ offset) for i in range(size)]) for offset in range(1, size)
    ]
    ordered = jnp.take(jnp.stack(received), jnp.bitwise_xor(me, jnp.arange(size, dtype=me.dtype)), axis=0)
    return ordered.reshape(size * value.shape[0], *value.shape[1:])


def conv_forward(padded, kernel, row_count):
    summed = jnp.zeros((row_count, padded.shape[1]), jnp.float32)
    for offset in range(kernel.shape[0]):
        summed = summed + kernel[offset].astype(jnp.float32) * padded[
            offset : offset + row_count
        ].astype(jnp.float32)
    return summed


def conv_transpose(padded, kernel, row_count):
    length = kernel.shape[0]
    summed = jnp.zeros((row_count, padded.shape[1]), jnp.float32)
    for offset in range(length):
        start = length - 1 - offset
        summed = summed + kernel[offset].astype(jnp.float32) * padded[start : start + row_count]
    return summed


def kernel_terms(padded, upstream, length, row_count):
    return jnp.stack(
        [
            jnp.sum(padded[offset : offset + row_count].astype(jnp.float32) * upstream, axis=0)
            for offset in range(length)
        ]
    )


def normalize(summed, norm_gain):
    square = jnp.mean(summed * summed, axis=-1, keepdims=True)
    return summed * lax.rsqrt(square + eps) * norm_gain


def slot_numbers(expert_ids, expert_count):
    onehot = (expert_ids[:, None] == jnp.arange(expert_count, dtype=jnp.int32)[None, :]).astype(
        jnp.int32
    )
    ranks = jnp.cumsum(onehot, axis=0) - onehot
    return jnp.sum(ranks * onehot, axis=1)


def gate_values(normed_b, router, first_ids, second_ids):
    logits = jnp.dot(normed_b, router, preferred_element_type=jnp.float32)
    columns = jnp.arange(router.shape[1], dtype=jnp.int32)[None, :]
    pick_diff = (first_ids[:, None] == columns).astype(jnp.float32) - (
        second_ids[:, None] == columns
    ).astype(jnp.float32)
    gate_one = jax.nn.sigmoid(jnp.sum(logits * pick_diff, axis=1))
    return (gate_one, 1.0 - gate_one, pick_diff)


def swish_parts(pre_act):
    squash = jax.nn.sigmoid(pre_act)
    return (pre_act * squash, squash * (1.0 + pre_act * (1.0 - squash)))


def gate_backward(upstream, out_one, out_two, gate_one, gate_two, pick_diff, normed_b, router):
    grad_gap = (
        (jnp.sum(upstream * out_one, axis=1) - jnp.sum(upstream * out_two, axis=1))
        * gate_one
        * gate_two
    )
    grad_logits = (grad_gap[:, None] * pick_diff).astype(jnp.bfloat16)
    router_term = jnp.dot(normed_b.T, grad_logits, preferred_element_type=jnp.float32)
    normed_term = jnp.dot(grad_logits, router.T, preferred_element_type=jnp.float32)
    return (router_term, normed_term)


def body(frames, kernel, norm_gain, router, experts, w_in, w_out, cotangent):
    inputs_dev = frames[0]
    row_count = inputs_dev.shape[0]
    width = inputs_dev.shape[1]
    length = kernel.shape[0]
    half_width = length // 2
    expert_count = router.shape[1]
    top_count = experts.shape[2]
    capacity = 2 * row_count * top_count // expert_count
    seq_size = lax.psum(1, SEQ)
    in_weights = w_in[0]
    out_weights = w_out[0]
    padded = padded_2(inputs_dev, SEQ, seq_size, half_width)
    summed = inputs_dev.astype(jnp.float32) + conv_forward(padded, kernel, row_count)
    normed_b = normalize(summed, norm_gain).astype(jnp.bfloat16)
    choice_ids = experts[0]
    gate_one, gate_two, pick_diff = gate_values(
        normed_b, router, choice_ids[:, 0], choice_ids[:, 1]
    )
    flat_ids = choice_ids.reshape(-1)
    slot_index = slot_numbers(flat_ids, expert_count)
    position = flat_ids * capacity + slot_index
    dispatch_table = (
        lax.broadcasted_iota(jnp.int32, (expert_count * capacity, flat_ids.shape[0]), 0)
        == position[None, :]
    ).astype(jnp.bfloat16)

    upstream = cotangent[0].astype(jnp.float32)
    repeated = jnp.repeat(normed_b, top_count, axis=0)
    grad_assigned = jnp.stack([gate_one[:, None] * upstream, gate_two[:, None] * upstream], axis=1)
    grad_values = grad_assigned.reshape(row_count * top_count, width).astype(jnp.bfloat16)
    both = jnp.concatenate([repeated, grad_values], axis=1)
    packed = jnp.dot(dispatch_table, both, preferred_element_type=jnp.float32).astype(jnp.bfloat16)
    packed = packed.reshape(expert_count, capacity, 2 * width)
    arrived = lax.all_to_all(packed, GRP, split_axis=0, concat_axis=0, tiled=True)
    in_all = gather_slices(in_weights)
    out_all = gather_slices(out_weights)
    slices = in_all.shape[0] * in_all.shape[1]
    hid = in_weights.shape[1]
    in_all = in_all.reshape(slices, width, hid)
    out_all = out_all.reshape(slices, hid, width)
    flat = arrived.reshape(-1, 2 * width)
    flat_rows = flat[:, :width]
    flat_grads = flat[:, width:]
    n_rows = flat.shape[0]

    in_cat = jnp.transpose(in_all, (1, 0, 2)).reshape(width, slices * hid)
    out_cat = out_all.reshape(slices * hid, width)
    pre_act = jnp.dot(flat_rows, in_cat, preferred_element_type=jnp.float32)
    hidden_f, slope = swish_parts(pre_act)
    hidden = hidden_f.astype(jnp.bfloat16)
    grad_hidden = jnp.dot(flat_grads, out_cat.T, preferred_element_type=jnp.float32)
    grad_pre = (grad_hidden * slope).astype(jnp.bfloat16)
    out_term = jnp.dot(hidden.T, flat_grads, preferred_element_type=jnp.float32)
    in_term = jnp.dot(flat_rows.T, grad_pre, preferred_element_type=jnp.float32)
    hidden, grad_pre, in_term, out_term = lax.optimization_barrier((hidden, grad_pre, in_term, out_term))
    hidden_s = hidden.reshape(n_rows, slices, hid)
    partial_rows = jnp.einsum(
        "rsh,shd->srd", hidden_s, out_all, preferred_element_type=jnp.float32
    ).astype(jnp.bfloat16)
    expert_rows = partial_rows[0].astype(jnp.float32)
    for member in range(1, slices):
        expert_rows = expert_rows + partial_rows[member].astype(jnp.float32)
    grad_parts = jnp.einsum(
        "rsh,sdh->srd", grad_pre.reshape(n_rows, slices, hid), in_all,
        preferred_element_type=jnp.float32,
    ).astype(jnp.bfloat16)
    grad_rows = grad_parts[0].astype(jnp.float32)
    for member in range(1, slices):
        grad_rows = grad_rows + grad_parts[member].astype(jnp.float32)

    in_term = jnp.transpose(in_term.reshape(width, slices, hid), (1, 0, 2))
    in_term = in_term.reshape(2, 2, width, hid)
    out_term = out_term.reshape(2, 2, width, hid)
    terms = jnp.concatenate([in_term, out_term], axis=3).astype(jnp.bfloat16)
    pair_terms = terms[0].astype(jnp.float32) + swap(terms[1], "c").astype(jnp.float32)
    own_terms = pair_terms[0] + swap(pair_terms[1].astype(jnp.bfloat16), "xl").astype(jnp.float32)
    mine = own_terms.astype(jnp.bfloat16)
    other = swap(mine, "dp")
    dp_first = lax.axis_index("dp") == 0
    first = jnp.where(dp_first, mine, other).astype(jnp.float32)
    second = jnp.where(dp_first, other, mine).astype(jnp.float32)
    grad_terms = first + second
    grad_in = grad_terms[:, :hid]
    grad_out = grad_terms[:, hid:].reshape(hid, width)

    back = jnp.concatenate([expert_rows, grad_rows], axis=1).astype(jnp.bfloat16)
    back = back.reshape(expert_count, capacity, 2 * width)
    totals = lax.all_to_all(back, GRP, split_axis=0, concat_axis=0, tiled=True)
    totals = totals.reshape(expert_count * capacity, 2 * width)
    picked = jnp.take(totals, position, axis=0).astype(jnp.float32)
    picked = picked.reshape(row_count, top_count, 2 * width)
    out_one = picked[:, 0, :width]
    out_two = picked[:, 1, :width]
    normed_grads = picked[:, 0, width:] + picked[:, 1, width:]

    mixed = (summed + gate_one[:, None] * out_one + gate_two[:, None] * out_two).astype(
        jnp.bfloat16
    )
    router_term, normed_term = gate_backward(
        upstream, out_one, out_two, gate_one, gate_two, pick_diff, normed_b, router
    )
    pullback = jax.vjp(normalize, summed, norm_gain)[1]
    summed_grad, gain_term = pullback(normed_grads + normed_term)
    upstream_total = upstream + summed_grad
    padded_grad = padded_2(
        upstream_total.astype(jnp.bfloat16), SEQ, seq_size, half_width
    ).astype(upstream_total.dtype)
    grad_frames = (upstream_total + conv_transpose(padded_grad, kernel, row_count)).astype(
        jnp.bfloat16
    )
    kernel_term = kernel_terms(padded, upstream_total, length, row_count)
    small = jnp.concatenate([kernel_term, gain_term[None, :], router_term.T], axis=0)
    rows_small = small.shape[0]
    chunk = reduce_scatter(small, "z", 8)
    chunk = reduce_scatter(chunk, "y", 4)
    for axis in ("c", "xl", "dp"):
        chunk = chunk + swap(chunk, axis)
    chunk = all_gather(chunk, "y", 4)
    small = all_gather(chunk, "z", 8).reshape(rows_small, -1)
    grad_kernel = small[:length]
    grad_gain = small[length]
    grad_router = small[length + 1 :].T
    return (
        mixed[None],
        grad_frames[None],
        grad_kernel,
        grad_gain,
        grad_router,
        grad_in[None],
        grad_out[None],
    )


def solution(mesh):
    split_mesh = Mesh(mesh.devices.reshape(8, 4, 2, 2, 2), SEQ + ("dp",))
    return jax.shard_map(
        body,
        mesh=split_mesh,
        in_specs=(
            P("dp", SEQ, None),
            P(),
            P(),
            P(),
            P("dp", SEQ, None),
            P(SEQ, None, None),
            P(SEQ, None, None),
            P("dp", SEQ, None),
        ),
        out_specs=(
            P("dp", SEQ, None),
            P("dp", SEQ, None),
            P(),
            P(),
            P(),
            P(SEQ, None, None),
            P(SEQ, None, None),
        ),
        check_vma=False,
    )
```

```python
import jax
import jax.numpy as jnp
from jax import lax
from jax.sharding import Mesh
from jax.sharding import PartitionSpec as P

eps = 1e-06

SEQ = ("z", "y", "xl", "c")
GRP = ("z", "y")


def padded_2(shard, axis, size, width):
    length = shard.shape[0]
    up = [(i, (i + 1) % size) for i in range(size - 1)]
    down = [(j, i) for i, j in up]
    last = lax.slice_in_dim(shard, length - width, length, axis=0)
    initial = lax.slice_in_dim(shard, 0, width, axis=0)
    before = lax.ppermute(last, axis, up)
    after = lax.ppermute(initial, axis, down)
    return jnp.concatenate([before, shard, after], axis=0)


def swap(value, axis):
    return lax.ppermute(value, axis, [(0, 1), (1, 0)])


def gather_slices(weights):
    pair = jnp.stack([weights, swap(weights, "xl")])
    return jnp.stack([pair, swap(pair, "c")])


def group_sum(value, axes, size):
    received = [value] + [
        lax.ppermute(value, axes, [(i, i ^ offset) for i in range(size)]) for offset in range(1, size)
    ]
    me = lax.axis_index(axes)
    stacked = jnp.stack(received)
    ordered = jnp.take(stacked, jnp.bitwise_xor(me, jnp.arange(size, dtype=me.dtype)), axis=0)
    total = ordered[0]
    for member in range(1, size):
        total = total + ordered[member]
    return total


def reduce_weight_terms(terms):
    pair_terms = terms[0].astype(jnp.float32) + swap(terms[1], "c").astype(jnp.float32)
    own_terms = pair_terms[0] + swap(pair_terms[1].astype(jnp.bfloat16), "xl").astype(jnp.float32)
    mine = own_terms.astype(jnp.bfloat16)
    other = swap(mine, "dp")
    dp_first = lax.axis_index("dp") == 0
    first = jnp.where(dp_first, mine, other).astype(jnp.float32)
    second = jnp.where(dp_first, other, mine).astype(jnp.float32)
    return first + second


def reduce_scatter(value, axis, size):
    chunks = value.reshape(size, value.shape[0] // size, *value.shape[1:])
    me = lax.axis_index(axis)
    total = lax.dynamic_index_in_dim(chunks, me, axis=0, keepdims=False)
    for offset in range(1, size):
        piece = lax.dynamic_index_in_dim(chunks, jnp.bitwise_xor(me, offset), axis=0, keepdims=False)
        total = total + lax.ppermute(piece, axis, [(i, i ^ offset) for i in range(size)])
    return total


def all_gather(value, axis, size):
    me = lax.axis_index(axis)
    received = [value] + [
        lax.ppermute(value, axis, [(i, i ^ offset) for i in range(size)]) for offset in range(1, size)
    ]
    ordered = jnp.take(jnp.stack(received), jnp.bitwise_xor(me, jnp.arange(size, dtype=me.dtype)), axis=0)
    return ordered.reshape(size * value.shape[0], *value.shape[1:])


def conv_forward(padded, kernel, row_count):
    summed = jnp.zeros((row_count, padded.shape[1]), jnp.float32)
    for offset in range(kernel.shape[0]):
        summed = summed + kernel[offset].astype(jnp.float32) * padded[
            offset : offset + row_count
        ].astype(jnp.float32)
    return summed


def conv_transpose(padded, kernel, row_count):
    length = kernel.shape[0]
    summed = jnp.zeros((row_count, padded.shape[1]), jnp.float32)
    for offset in range(length):
        start = length - 1 - offset
        summed = summed + kernel[offset].astype(jnp.float32) * padded[start : start + row_count]
    return summed


def kernel_terms(padded, upstream, length, row_count):
    return jnp.stack(
        [
            jnp.sum(padded[offset : offset + row_count].astype(jnp.float32) * upstream, axis=0)
            for offset in range(length)
        ]
    )


def normalize(summed, norm_gain):
    square = jnp.mean(summed * summed, axis=-1, keepdims=True)
    return summed * lax.rsqrt(square + eps) * norm_gain


def slot_numbers(expert_ids, expert_count):
    onehot = (expert_ids[:, None] == jnp.arange(expert_count, dtype=jnp.int32)[None, :]).astype(
        jnp.int32
    )
    ranks = jnp.cumsum(onehot, axis=0) - onehot
    return jnp.sum(ranks * onehot, axis=1)


def gate_values(normed_b, router, first_ids, second_ids):
    logits = jnp.dot(normed_b, router, preferred_element_type=jnp.float32)
    columns = jnp.arange(router.shape[1], dtype=jnp.int32)[None, :]
    pick_diff = (first_ids[:, None] == columns).astype(jnp.float32) - (
        second_ids[:, None] == columns
    ).astype(jnp.float32)
    gate_one = jax.nn.sigmoid(jnp.sum(logits * pick_diff, axis=1))
    return (gate_one, 1.0 - gate_one, pick_diff)


def swish_parts(pre_act):
    squash = jax.nn.sigmoid(pre_act)
    return (pre_act * squash, squash * (1.0 + pre_act * (1.0 - squash)))


def gate_backward(upstream, out_one, out_two, gate_one, gate_two, pick_diff, normed_b, router):
    grad_gap = (
        (jnp.sum(upstream * out_one, axis=1) - jnp.sum(upstream * out_two, axis=1))
        * gate_one
        * gate_two
    )
    grad_logits = (grad_gap[:, None] * pick_diff).astype(jnp.bfloat16)
    router_term = jnp.dot(normed_b.T, grad_logits, preferred_element_type=jnp.float32)
    normed_term = jnp.dot(grad_logits, router.T, preferred_element_type=jnp.float32)
    return (router_term, normed_term)


def body(frames, kernel, norm_gain, router, experts, w_in, w_out, cotangent):
    inputs_dev = frames[0]
    row_count = inputs_dev.shape[0]
    width = inputs_dev.shape[1]
    length = kernel.shape[0]
    half_width = length // 2
    expert_count = router.shape[1]
    top_count = experts.shape[2]
    capacity = 2 * row_count * top_count // expert_count
    seq_size = lax.psum(1, SEQ)
    in_weights = w_in[0]
    out_weights = w_out[0]
    padded = padded_2(inputs_dev, SEQ, seq_size, half_width)
    summed = inputs_dev.astype(jnp.float32) + conv_forward(padded, kernel, row_count)
    normed_b = normalize(summed, norm_gain).astype(jnp.bfloat16)
    choice_ids = experts[0]
    gate_one, gate_two, pick_diff = gate_values(
        normed_b, router, choice_ids[:, 0], choice_ids[:, 1]
    )
    flat_ids = choice_ids.reshape(-1)
    slot_index = slot_numbers(flat_ids, expert_count)
    position = flat_ids * capacity + slot_index
    dispatch_table = (
        lax.broadcasted_iota(jnp.int32, (expert_count * capacity, flat_ids.shape[0]), 0)
        == position[None, :]
    ).astype(jnp.bfloat16)

    upstream = cotangent[0].astype(jnp.float32)
    repeated = jnp.repeat(normed_b, top_count, axis=0)
    grad_assigned = jnp.stack([gate_one[:, None] * upstream, gate_two[:, None] * upstream], axis=1)
    grad_values = grad_assigned.reshape(row_count * top_count, width).astype(jnp.bfloat16)
    both = jnp.concatenate([repeated, grad_values], axis=1)
    packed = jnp.dot(dispatch_table, both, preferred_element_type=jnp.float32).astype(jnp.bfloat16)
    packed = packed.reshape(expert_count, capacity, 2 * width)
    arrived = lax.all_to_all(packed, GRP, split_axis=0, concat_axis=0, tiled=True)
    in_all = gather_slices(in_weights)
    out_all = gather_slices(out_weights)
    slices = in_all.shape[0] * in_all.shape[1]
    hid = in_weights.shape[1]
    in_all = in_all.reshape(slices, width, hid)
    out_all = out_all.reshape(slices, hid, width)
    flat = arrived.reshape(-1, 2 * width)
    flat_rows = flat[:, :width]
    flat_grads = flat[:, width:]
    n_rows = flat.shape[0]

    in_cat = jnp.transpose(in_all, (1, 0, 2)).reshape(width, slices * hid)
    out_cat = out_all.reshape(slices * hid, width)
    pre_act = jnp.dot(flat_rows, in_cat, preferred_element_type=jnp.float32)
    hidden_f, slope = swish_parts(pre_act)
    hidden = hidden_f.astype(jnp.bfloat16)
    grad_hidden = jnp.dot(flat_grads, out_cat.T, preferred_element_type=jnp.float32)
    grad_pre = (grad_hidden * slope).astype(jnp.bfloat16)
    out_term = jnp.dot(hidden.T, flat_grads, preferred_element_type=jnp.float32)
    in_term = jnp.dot(flat_rows.T, grad_pre, preferred_element_type=jnp.float32)
    hidden, grad_pre, in_term, out_term = lax.optimization_barrier((hidden, grad_pre, in_term, out_term))
    hidden_s = hidden.reshape(n_rows, slices, hid)
    partial_rows = jnp.einsum(
        "rsh,shd->srd", hidden_s, out_all, preferred_element_type=jnp.float32
    ).astype(jnp.bfloat16)
    expert_rows = partial_rows[0].astype(jnp.float32)
    for member in range(1, slices):
        expert_rows = expert_rows + partial_rows[member].astype(jnp.float32)
    grad_parts = jnp.einsum(
        "rsh,sdh->srd", grad_pre.reshape(n_rows, slices, hid), in_all,
        preferred_element_type=jnp.float32,
    ).astype(jnp.bfloat16)
    grad_rows = grad_parts[0].astype(jnp.float32)
    for member in range(1, slices):
        grad_rows = grad_rows + grad_parts[member].astype(jnp.float32)

    in_term = jnp.transpose(in_term.reshape(width, slices, hid), (1, 0, 2))
    in_term = in_term.reshape(2, 2, width, hid)
    out_term = out_term.reshape(2, 2, width, hid)
    grad_in = reduce_weight_terms(in_term.astype(jnp.bfloat16))
    grad_out = reduce_weight_terms(out_term.astype(jnp.bfloat16)).reshape(hid, width)

    back = jnp.concatenate([expert_rows, grad_rows], axis=1).astype(jnp.bfloat16)
    back = back.reshape(expert_count, capacity, 2 * width)
    totals = lax.all_to_all(back, GRP, split_axis=0, concat_axis=0, tiled=True)
    totals = totals.reshape(expert_count * capacity, 2 * width)
    picked = jnp.take(totals, position, axis=0).astype(jnp.float32)
    picked = picked.reshape(row_count, top_count, 2 * width)
    out_one = picked[:, 0, :width]
    out_two = picked[:, 1, :width]
    normed_grads = picked[:, 0, width:] + picked[:, 1, width:]

    mixed = (summed + gate_one[:, None] * out_one + gate_two[:, None] * out_two).astype(
        jnp.bfloat16
    )
    router_term, normed_term = gate_backward(
        upstream, out_one, out_two, gate_one, gate_two, pick_diff, normed_b, router
    )
    pullback = jax.vjp(normalize, summed, norm_gain)[1]
    summed_grad, gain_term = pullback(normed_grads + normed_term)
    upstream_total = upstream + summed_grad
    padded_grad = padded_2(
        upstream_total.astype(jnp.bfloat16), SEQ, seq_size, half_width
    ).astype(upstream_total.dtype)
    grad_frames = (upstream_total + conv_transpose(padded_grad, kernel, row_count)).astype(
        jnp.bfloat16
    )
    kernel_term = kernel_terms(padded, upstream_total, length, row_count)
    small = jnp.concatenate([kernel_term, gain_term[None, :], router_term.T], axis=0)
    rows_small = small.shape[0]
    chunk = reduce_scatter(small, "z", 8)
    chunk = reduce_scatter(chunk, "y", 4)
    for axis in ("c", "xl", "dp"):
        chunk = chunk + swap(chunk, axis)
    chunk = all_gather(chunk, "y", 4)
    small = all_gather(chunk, "z", 8).reshape(rows_small, -1)
    grad_kernel = small[:length]
    grad_gain = small[length]
    grad_router = small[length + 1 :].T
    return (
        mixed[None],
        grad_frames[None],
        grad_kernel,
        grad_gain,
        grad_router,
        grad_in[None],
        grad_out[None],
    )


def solution(mesh):
    split_mesh = Mesh(mesh.devices.reshape(8, 4, 2, 2, 2), SEQ + ("dp",))
    return jax.shard_map(
        body,
        mesh=split_mesh,
        in_specs=(
            P("dp", SEQ, None),
            P(),
            P(),
            P(),
            P("dp", SEQ, None),
            P(SEQ, None, None),
            P(SEQ, None, None),
            P("dp", SEQ, None),
        ),
        out_specs=(
            P("dp", SEQ, None),
            P("dp", SEQ, None),
            P(),
            P(),
            P(),
            P(SEQ, None, None),
            P(SEQ, None, None),
        ),
        check_vma=False,
    )
```

```python
import jax
import jax.numpy as jnp
from jax import lax
from jax.sharding import Mesh
from jax.sharding import PartitionSpec as P

eps = 1e-06

SEQ = ("z", "y", "xl", "c")
GRP = ("z", "y")


def padded_2(shard, axis, size, width):
    length = shard.shape[0]
    up = [(i, (i + 1) % size) for i in range(size - 1)]
    down = [(j, i) for i, j in up]
    last = lax.slice_in_dim(shard, length - width, length, axis=0)
    initial = lax.slice_in_dim(shard, 0, width, axis=0)
    before = lax.ppermute(last, axis, up)
    after = lax.ppermute(initial, axis, down)
    return jnp.concatenate([before, shard, after], axis=0)


def swap(value, axis):
    return lax.ppermute(value, axis, [(0, 1), (1, 0)])


def gather_slices(weights):
    pair = jnp.stack([weights, swap(weights, "xl")])
    return jnp.stack([pair, swap(pair, "c")])


def group_sum(value, axes, size):
    received = [value] + [
        lax.ppermute(value, axes, [(i, i ^ offset) for i in range(size)]) for offset in range(1, size)
    ]
    me = lax.axis_index(axes)
    stacked = jnp.stack(received)
    ordered = jnp.take(stacked, jnp.bitwise_xor(me, jnp.arange(size, dtype=me.dtype)), axis=0)
    total = ordered[0]
    for member in range(1, size):
        total = total + ordered[member]
    return total


def reduce_weight_terms(terms):
    pair_terms = terms[0].astype(jnp.float32) + swap(terms[1], "c").astype(jnp.float32)
    own_terms = pair_terms[0] + swap(pair_terms[1].astype(jnp.bfloat16), "xl").astype(jnp.float32)
    mine = own_terms.astype(jnp.bfloat16)
    other = swap(mine, "dp")
    dp_first = lax.axis_index("dp") == 0
    first = jnp.where(dp_first, mine, other).astype(jnp.float32)
    second = jnp.where(dp_first, other, mine).astype(jnp.float32)
    return first + second


def reduce_scatter(value, axis, size):
    chunks = value.reshape(size, value.shape[0] // size, *value.shape[1:])
    me = lax.axis_index(axis)
    total = lax.dynamic_index_in_dim(chunks, me, axis=0, keepdims=False)
    for offset in range(1, size):
        piece = lax.dynamic_index_in_dim(chunks, jnp.bitwise_xor(me, offset), axis=0, keepdims=False)
        total = total + lax.ppermute(piece, axis, [(i, i ^ offset) for i in range(size)])
    return total


def all_gather(value, axis, size):
    me = lax.axis_index(axis)
    received = [value] + [
        lax.ppermute(value, axis, [(i, i ^ offset) for i in range(size)]) for offset in range(1, size)
    ]
    ordered = jnp.take(jnp.stack(received), jnp.bitwise_xor(me, jnp.arange(size, dtype=me.dtype)), axis=0)
    return ordered.reshape(size * value.shape[0], *value.shape[1:])


def conv_forward(padded, kernel, row_count):
    summed = jnp.zeros((row_count, padded.shape[1]), jnp.float32)
    for offset in range(kernel.shape[0]):
        summed = summed + kernel[offset].astype(jnp.float32) * padded[
            offset : offset + row_count
        ].astype(jnp.float32)
    return summed


def conv_transpose(padded, kernel, row_count):
    length = kernel.shape[0]
    summed = jnp.zeros((row_count, padded.shape[1]), jnp.float32)
    for offset in range(length):
        start = length - 1 - offset
        summed = summed + kernel[offset].astype(jnp.float32) * padded[start : start + row_count]
    return summed


def kernel_terms(padded, upstream, length, row_count):
    return jnp.stack(
        [
            jnp.sum(padded[offset : offset + row_count].astype(jnp.float32) * upstream, axis=0)
            for offset in range(length)
        ]
    )


def normalize(summed, norm_gain):
    square = jnp.mean(summed * summed, axis=-1, keepdims=True)
    return summed * lax.rsqrt(square + eps) * norm_gain


def slot_numbers(expert_ids, expert_count):
    onehot = (expert_ids[:, None] == jnp.arange(expert_count, dtype=jnp.int32)[None, :]).astype(
        jnp.int32
    )
    ranks = jnp.cumsum(onehot, axis=0) - onehot
    return jnp.sum(ranks * onehot, axis=1)


def gate_values(normed_b, router, first_ids, second_ids):
    logits = jnp.dot(normed_b, router, preferred_element_type=jnp.float32)
    columns = jnp.arange(router.shape[1], dtype=jnp.int32)[None, :]
    pick_diff = (first_ids[:, None] == columns).astype(jnp.float32) - (
        second_ids[:, None] == columns
    ).astype(jnp.float32)
    gate_one = jax.nn.sigmoid(jnp.sum(logits * pick_diff, axis=1))
    return (gate_one, 1.0 - gate_one, pick_diff)


def swish_parts(pre_act):
    squash = jax.nn.sigmoid(pre_act)
    return (pre_act * squash, squash * (1.0 + pre_act * (1.0 - squash)))


def gate_backward(upstream, out_one, out_two, gate_one, gate_two, pick_diff, normed_b, router):
    grad_gap = (
        (jnp.sum(upstream * out_one, axis=1) - jnp.sum(upstream * out_two, axis=1))
        * gate_one
        * gate_two
    )
    grad_logits = (grad_gap[:, None] * pick_diff).astype(jnp.bfloat16)
    router_term = jnp.dot(normed_b.T, grad_logits, preferred_element_type=jnp.float32)
    normed_term = jnp.dot(grad_logits, router.T, preferred_element_type=jnp.float32)
    return (router_term, normed_term)


def body(frames, kernel, norm_gain, router, experts, w_in, w_out, cotangent):
    inputs_dev = frames[0]
    row_count = inputs_dev.shape[0]
    width = inputs_dev.shape[1]
    length = kernel.shape[0]
    half_width = length // 2
    expert_count = router.shape[1]
    top_count = experts.shape[2]
    capacity = 2 * row_count * top_count // expert_count
    seq_size = lax.psum(1, SEQ)
    in_weights = w_in[0]
    out_weights = w_out[0]
    padded = padded_2(inputs_dev, SEQ, seq_size, half_width)
    summed = inputs_dev.astype(jnp.float32) + conv_forward(padded, kernel, row_count)
    normed_b = normalize(summed, norm_gain).astype(jnp.bfloat16)
    choice_ids = experts[0]
    gate_one, gate_two, pick_diff = gate_values(
        normed_b, router, choice_ids[:, 0], choice_ids[:, 1]
    )
    flat_ids = choice_ids.reshape(-1)
    slot_index = slot_numbers(flat_ids, expert_count)
    position = flat_ids * capacity + slot_index
    dispatch_table = (
        lax.broadcasted_iota(jnp.int32, (expert_count * capacity, flat_ids.shape[0]), 0)
        == position[None, :]
    ).astype(jnp.bfloat16)

    upstream = cotangent[0].astype(jnp.float32)
    repeated = jnp.repeat(normed_b, top_count, axis=0)
    grad_assigned = jnp.stack([gate_one[:, None] * upstream, gate_two[:, None] * upstream], axis=1)
    grad_values = grad_assigned.reshape(row_count * top_count, width).astype(jnp.bfloat16)
    both = jnp.concatenate([repeated, grad_values], axis=1)
    packed = jnp.dot(dispatch_table, both, preferred_element_type=jnp.float32).astype(jnp.bfloat16)
    packed = packed.reshape(expert_count, capacity, 2 * width)
    arrived = lax.all_to_all(packed, GRP, split_axis=0, concat_axis=0, tiled=True)
    in_all = gather_slices(in_weights)
    out_all = gather_slices(out_weights)
    slices = in_all.shape[0] * in_all.shape[1]
    hid = in_weights.shape[1]
    in_all = in_all.reshape(slices, width, hid)
    out_all = out_all.reshape(slices, hid, width)
    flat = arrived.reshape(-1, 2 * width)
    flat_rows = flat[:, :width]
    flat_grads = flat[:, width:]
    n_rows = flat.shape[0]

    in_cat = jnp.transpose(in_all, (1, 0, 2)).reshape(width, slices * hid)
    out_cat = out_all.reshape(slices * hid, width)
    pre_act = jnp.dot(flat_rows, in_cat, preferred_element_type=jnp.float32)
    hidden_f, slope = swish_parts(pre_act)
    hidden = hidden_f.astype(jnp.bfloat16)
    grad_hidden = jnp.dot(flat_grads, out_cat.T, preferred_element_type=jnp.float32)
    grad_pre = (grad_hidden * slope).astype(jnp.bfloat16)
    out_term = jnp.dot(hidden.T, flat_grads, preferred_element_type=jnp.float32)
    in_term = jnp.dot(flat_rows.T, grad_pre, preferred_element_type=jnp.float32)
    hidden, grad_pre, in_term, out_term = lax.optimization_barrier((hidden, grad_pre, in_term, out_term))
    hidden_s = hidden.reshape(n_rows, slices, hid)
    partial_rows = jnp.einsum(
        "rsh,shd->srd", hidden_s, out_all, preferred_element_type=jnp.float32
    ).astype(jnp.bfloat16)
    expert_rows = partial_rows[0].astype(jnp.float32)
    for member in range(1, slices):
        expert_rows = expert_rows + partial_rows[member].astype(jnp.float32)
    grad_parts = jnp.einsum(
        "rsh,sdh->srd", grad_pre.reshape(n_rows, slices, hid), in_all,
        preferred_element_type=jnp.float32,
    ).astype(jnp.bfloat16)
    grad_rows = grad_parts[0].astype(jnp.float32)
    for member in range(1, slices):
        grad_rows = grad_rows + grad_parts[member].astype(jnp.float32)

    in_term = jnp.transpose(in_term.reshape(width, slices, hid), (1, 0, 2))
    in_term = in_term.reshape(2, 2, width, hid)
    out_term = out_term.reshape(2, 2, width, hid)
    grad_in = reduce_weight_terms(in_term.astype(jnp.bfloat16))
    grad_out = reduce_weight_terms(out_term.astype(jnp.bfloat16)).reshape(hid, width)

    back = jnp.concatenate([expert_rows, grad_rows], axis=1).astype(jnp.bfloat16)
    back = back.reshape(expert_count, capacity, 2 * width)
    totals = lax.all_to_all(back, GRP, split_axis=0, concat_axis=0, tiled=True)
    totals = totals.reshape(expert_count * capacity, 2 * width)
    picked = jnp.take(totals, position, axis=0).astype(jnp.float32)
    picked = picked.reshape(row_count, top_count, 2 * width)
    out_one = picked[:, 0, :width]
    out_two = picked[:, 1, :width]
    normed_grads = picked[:, 0, width:] + picked[:, 1, width:]

    mixed = (summed + gate_one[:, None] * out_one + gate_two[:, None] * out_two).astype(
        jnp.bfloat16
    )
    router_term, normed_term = gate_backward(
        upstream, out_one, out_two, gate_one, gate_two, pick_diff, normed_b, router
    )
    pullback = jax.vjp(normalize, summed, norm_gain)[1]
    summed_grad, gain_term = pullback(normed_grads + normed_term)
    upstream_total = upstream + summed_grad
    padded_grad = padded_2(
        upstream_total.astype(jnp.bfloat16), SEQ, seq_size, half_width
    ).astype(upstream_total.dtype)
    grad_frames = (upstream_total + conv_transpose(padded_grad, kernel, row_count)).astype(
        jnp.bfloat16
    )
    kernel_term = kernel_terms(padded, upstream_total, length, row_count)
    small = jnp.concatenate([kernel_term, gain_term[None, :], router_term.T], axis=0)
    rows_small = small.shape[0]
    for axis in ("c", "xl", "dp"):
        small = small + swap(small, axis)
    chunk = reduce_scatter(small, "z", 8)
    chunk = reduce_scatter(chunk, "y", 4)
    chunk = all_gather(chunk, "y", 4)
    small = all_gather(chunk, "z", 8).reshape(rows_small, -1)
    grad_kernel = small[:length]
    grad_gain = small[length]
    grad_router = small[length + 1 :].T
    return (
        mixed[None],
        grad_frames[None],
        grad_kernel,
        grad_gain,
        grad_router,
        grad_in[None],
        grad_out[None],
    )


def solution(mesh):
    split_mesh = Mesh(mesh.devices.reshape(8, 4, 2, 2, 2), SEQ + ("dp",))
    return jax.shard_map(
        body,
        mesh=split_mesh,
        in_specs=(
            P("dp", SEQ, None),
            P(),
            P(),
            P(),
            P("dp", SEQ, None),
            P(SEQ, None, None),
            P(SEQ, None, None),
            P("dp", SEQ, None),
        ),
        out_specs=(
            P("dp", SEQ, None),
            P("dp", SEQ, None),
            P(),
            P(),
            P(),
            P(SEQ, None, None),
            P(SEQ, None, None),
        ),
        check_vma=False,
    )
```

```python
import jax
import jax.numpy as jnp
from jax import lax
from jax.sharding import Mesh
from jax.sharding import PartitionSpec as P


eps = 1e-06

SEQ = ("z", "y", "xl", "c")
GRP = ("z", "y")


def padded_2(shard, axis, size, width):
    length = shard.shape[0]
    up = [(i, (i + 1) % size) for i in range(size - 1)]
    down = [(j, i) for i, j in up]
    last = lax.slice_in_dim(shard, length - width, length, axis=0)
    initial = lax.slice_in_dim(shard, 0, width, axis=0)
    before = lax.ppermute(last, axis, up)
    after = lax.ppermute(initial, axis, down)
    return jnp.concatenate([before, shard, after], axis=0)


def swap(value, axis):
    return lax.ppermute(value, axis, [(0, 1), (1, 0)])


def gather_slices(weights):
    other_x = swap(weights, "xl")
    pair = jnp.stack([weights, other_x])
    return jnp.stack([pair, swap(pair, "c")])


def reduce_weight_terms(terms):
    pair_terms = terms[0].astype(jnp.float32) + swap(terms[1], "c").astype(jnp.float32)
    own_terms = pair_terms[0] + swap(pair_terms[1].astype(jnp.bfloat16), "xl").astype(jnp.float32)
    mine = own_terms.astype(jnp.bfloat16)
    other = swap(mine, "dp")
    dp_first = lax.axis_index("dp") == 0
    first = jnp.where(dp_first, mine, other).astype(jnp.float32)
    second = jnp.where(dp_first, other, mine).astype(jnp.float32)
    return first + second


def reduce_scatter(value, axis, size):
    chunks = value.reshape(size, value.shape[0] // size, *value.shape[1:])
    me = lax.axis_index(axis)
    total = lax.dynamic_index_in_dim(chunks, me, axis=0, keepdims=False)
    for offset in range(1, size):
        piece = lax.dynamic_index_in_dim(chunks, jnp.bitwise_xor(me, offset), axis=0, keepdims=False)
        total = total + lax.ppermute(piece, axis, [(i, i ^ offset) for i in range(size)])
    return total


def all_gather(value, axis, size):
    me = lax.axis_index(axis)
    received = [value] + [
        lax.ppermute(value, axis, [(i, i ^ offset) for i in range(size)]) for offset in range(1, size)
    ]
    ordered = jnp.take(jnp.stack(received), jnp.bitwise_xor(me, jnp.arange(size, dtype=me.dtype)), axis=0)
    return ordered.reshape(size * value.shape[0], *value.shape[1:])


def conv_forward(padded, kernel, row_count):
    summed = jnp.zeros((row_count, padded.shape[1]), jnp.float32)
    for offset in range(kernel.shape[0]):
        summed = summed + kernel[offset].astype(jnp.float32) * padded[
            offset : offset + row_count
        ].astype(jnp.float32)
    return summed


def conv_transpose(padded, kernel, row_count):
    length = kernel.shape[0]
    summed = jnp.zeros((row_count, padded.shape[1]), jnp.float32)
    for offset in range(length):
        start = length - 1 - offset
        summed = summed + kernel[offset].astype(jnp.float32) * padded[start : start + row_count]
    return summed


def kernel_terms(padded, upstream, length, row_count):
    return jnp.stack(
        [
            jnp.sum(padded[offset : offset + row_count].astype(jnp.float32) * upstream, axis=0)
            for offset in range(length)
        ]
    )


def normalize(summed, norm_gain):
    square = jnp.mean(summed * summed, axis=-1, keepdims=True)
    return summed * lax.rsqrt(square + eps) * norm_gain


def slot_numbers(expert_ids, expert_count):
    onehot = (expert_ids[:, None] == jnp.arange(expert_count, dtype=jnp.int32)[None, :]).astype(
        jnp.int32
    )
    ranks = jnp.cumsum(onehot, axis=0) - onehot
    return jnp.sum(ranks * onehot, axis=1)


def gate_values(normed_b, router, first_ids, second_ids):
    logits = jnp.dot(normed_b, router, preferred_element_type=jnp.float32)
    columns = jnp.arange(router.shape[1], dtype=jnp.int32)[None, :]
    pick_diff = (first_ids[:, None] == columns).astype(jnp.float32) - (
        second_ids[:, None] == columns
    ).astype(jnp.float32)
    gate_one = jax.nn.sigmoid(jnp.sum(logits * pick_diff, axis=1))
    return (gate_one, 1.0 - gate_one, pick_diff)


def swish_parts(pre_act):
    squash = jax.nn.sigmoid(pre_act)
    return (pre_act * squash, squash * (1.0 + pre_act * (1.0 - squash)))


def gate_backward(upstream, out_one, out_two, gate_one, gate_two, pick_diff, normed_b, router):
    grad_gap = (
        (jnp.sum(upstream * out_one, axis=1) - jnp.sum(upstream * out_two, axis=1))
        * gate_one
        * gate_two
    )
    grad_logits = (grad_gap[:, None] * pick_diff).astype(jnp.bfloat16)
    router_term = jnp.dot(normed_b.T, grad_logits, preferred_element_type=jnp.float32)
    normed_term = jnp.dot(grad_logits, router.T, preferred_element_type=jnp.float32)
    return (router_term, normed_term)


def body_inner(frames, kernel, norm_gain, router, experts, w_in, w_out, cotangent):
    inputs_dev = frames[0]
    row_count = inputs_dev.shape[0]
    width = inputs_dev.shape[1]
    length = kernel.shape[0]
    half_width = length // 2
    expert_count = router.shape[1]
    top_count = experts.shape[2]
    capacity = 2 * row_count * top_count // expert_count
    seq_size = lax.psum(1, SEQ)
    in_weights = w_in[0]
    out_weights = w_out[0]
    padded = padded_2(inputs_dev, SEQ, seq_size, half_width)
    summed = inputs_dev.astype(jnp.float32) + conv_forward(padded, kernel, row_count)
    normed_b = normalize(summed, norm_gain).astype(jnp.bfloat16)
    choice_ids = experts[0]
    gate_one, gate_two, pick_diff = gate_values(
        normed_b, router, choice_ids[:, 0], choice_ids[:, 1]
    )
    flat_ids = choice_ids.reshape(-1)
    slot_index = slot_numbers(flat_ids, expert_count)
    position = flat_ids * capacity + slot_index
    dispatch_table = (
        lax.broadcasted_iota(jnp.int32, (expert_count * capacity, flat_ids.shape[0]), 0)
        == position[None, :]
    ).astype(jnp.bfloat16)

    upstream = cotangent[0].astype(jnp.float32)
    repeated = jnp.repeat(normed_b, top_count, axis=0)
    grad_assigned = jnp.stack([gate_one[:, None] * upstream, gate_two[:, None] * upstream], axis=1)
    grad_values = grad_assigned.reshape(row_count * top_count, width).astype(jnp.bfloat16)
    both = jnp.concatenate([repeated, grad_values], axis=1)
    packed = jnp.dot(dispatch_table, both, preferred_element_type=jnp.float32).astype(jnp.bfloat16)
    packed = packed.reshape(expert_count, capacity, 2 * width)
    arrived = lax.all_to_all(packed, GRP, split_axis=0, concat_axis=0, tiled=True)
    in_all = gather_slices(in_weights)
    out_all = gather_slices(out_weights)
    slices = in_all.shape[0] * in_all.shape[1]
    hid = in_weights.shape[1]
    in_all = in_all.reshape(slices, width, hid)
    out_all = out_all.reshape(slices, hid, width)
    flat = arrived.reshape(-1, 2 * width)
    flat_rows = flat[:, :width]
    flat_grads = flat[:, width:]
    n_rows = flat.shape[0]

    in_cat = jnp.transpose(in_all, (1, 0, 2)).reshape(width, slices * hid)
    out_cat = out_all.reshape(slices * hid, width)
    pre_act = jnp.dot(flat_rows, in_cat, preferred_element_type=jnp.float32)
    hidden_f, slope = swish_parts(pre_act)
    hidden = hidden_f.astype(jnp.bfloat16)
    grad_hidden = jnp.dot(flat_grads, out_cat.T, preferred_element_type=jnp.float32)
    grad_pre = (grad_hidden * slope).astype(jnp.bfloat16)
    out_term = jnp.dot(hidden.T, flat_grads, preferred_element_type=jnp.float32)
    in_term = jnp.dot(flat_rows.T, grad_pre, preferred_element_type=jnp.float32)
    hidden, grad_pre, in_term, out_term = lax.optimization_barrier((hidden, grad_pre, in_term, out_term))
    hidden_s = hidden.reshape(n_rows, slices, hid)
    partial_rows = jnp.einsum(
        "rsh,shd->srd", hidden_s, out_all, preferred_element_type=jnp.float32
    ).astype(jnp.bfloat16)
    expert_rows = partial_rows[0].astype(jnp.float32)
    for member in range(1, slices):
        expert_rows = expert_rows + partial_rows[member].astype(jnp.float32)
    grad_parts = jnp.einsum(
        "rsh,sdh->srd", grad_pre.reshape(n_rows, slices, hid), in_all,
        preferred_element_type=jnp.float32,
    ).astype(jnp.bfloat16)
    grad_rows = grad_parts[0].astype(jnp.float32)
    for member in range(1, slices):
        grad_rows = grad_rows + grad_parts[member].astype(jnp.float32)

    in_term = jnp.transpose(in_term.reshape(width, slices, hid), (1, 0, 2))
    in_term = in_term.reshape(2, 2, width, hid)
    out_term = out_term.reshape(2, 2, width, hid)
    grad_in = reduce_weight_terms(in_term.astype(jnp.bfloat16))
    grad_out = reduce_weight_terms(out_term.astype(jnp.bfloat16)).reshape(hid, width)

    back = jnp.concatenate([expert_rows, grad_rows], axis=1).astype(jnp.bfloat16)
    back = back.reshape(expert_count, capacity, 2 * width)
    totals = lax.all_to_all(back, GRP, split_axis=0, concat_axis=0, tiled=True)
    totals = totals.reshape(expert_count * capacity, 2 * width)
    picked = jnp.take(totals, position, axis=0).astype(jnp.float32)
    picked = picked.reshape(row_count, top_count, 2 * width)
    out_one = picked[:, 0, :width]
    out_two = picked[:, 1, :width]
    normed_grads = picked[:, 0, width:] + picked[:, 1, width:]

    mixed = (summed + gate_one[:, None] * out_one + gate_two[:, None] * out_two).astype(
        jnp.bfloat16
    )
    router_term, normed_term = gate_backward(
        upstream, out_one, out_two, gate_one, gate_two, pick_diff, normed_b, router
    )
    pullback = jax.vjp(normalize, summed, norm_gain)[1]
    summed_grad, gain_term = pullback(normed_grads + normed_term)
    upstream_total = upstream + summed_grad
    padded_grad = padded_2(
        upstream_total.astype(jnp.bfloat16), SEQ, seq_size, half_width
    ).astype(upstream_total.dtype)
    grad_frames = (upstream_total + conv_transpose(padded_grad, kernel, row_count)).astype(
        jnp.bfloat16
    )
    kernel_term = kernel_terms(padded, upstream_total, length, row_count)
    small = jnp.concatenate([kernel_term, gain_term[None, :], router_term.T], axis=0)
    rows_small = small.shape[0]
    for axis in ("c", "xl", "dp"):
        small = small + swap(small, axis)
    chunk = reduce_scatter(small, "z", 8)
    chunk = reduce_scatter(chunk, "y", 4)
    chunk = all_gather(chunk, "y", 4)
    small = all_gather(chunk, "z", 8).reshape(rows_small, -1)
    grad_kernel = small[:length]
    grad_gain = small[length]
    grad_router = small[length + 1 :].T
    return (
        mixed[None],
        grad_frames[None],
        grad_kernel,
        grad_gain,
        grad_router,
        grad_in[None],
        grad_out[None],
    )


def solution(mesh):
    split_mesh = Mesh(mesh.devices.reshape(8, 4, 2, 2, 2), SEQ + ("dp",))
    return jax.shard_map(
        body_inner,
        mesh=split_mesh,
        in_specs=(
            P("dp", SEQ, None),
            P(),
            P(),
            P(),
            P("dp", SEQ, None),
            P(SEQ, None, None),
            P(SEQ, None, None),
            P("dp", SEQ, None),
        ),
        out_specs=(
            P("dp", SEQ, None),
            P("dp", SEQ, None),
            P(),
            P(),
            P(),
            P(SEQ, None, None),
            P(SEQ, None, None),
        ),
        check_vma=False,
    )
```
